256 devices in a mesh: seq: 32 (over z, y), head: 8 (over x, core).
Axes of the slice: x: 4, y: 4, z: 8, core: 2. Of those that a mesh axis runs over, the one named last changes fastest.
Arguments:
- queries: bfloat16 [8192, 4096], P('seq', 'head'), may hold values from -32 to 32
- key_rows: bfloat16 [8192, 4096], P('seq', 'head'), may hold values from -6 to 6
- value_rows: bfloat16 [8192, 4096], P('seq', 'head'), may hold values from -6 to 6
- out_weight: bfloat16 [4096, 4096], P('head', 'seq'), may hold values from -0.1875 to 0.1875
- grad_output: bfloat16 [8192, 4096], P('seq', 'head'), may hold values from -6 to 6
- cluster_ids: int32 [8192], P('seq'), may hold values from 0 to 31, as said below
- block_pattern: int32 [32, 2, 2], replicated, may hold values from 0 to 1, as said below
Outputs:
- layer_out: bfloat16 [8192, 4096], P('seq', 'head')
- grad_queries: bfloat16 [8192, 4096], P('seq', 'head')
- grad_keys: bfloat16 [8192, 4096], P('seq', 'head')
- grad_values: bfloat16 [8192, 4096], P('seq', 'head')
The draws below stay inside these ranges and needn't reach their ends.
Inputs may be any that keep to these rules, and one draw needn't show every extreme that they name: `cluster_ids`: every cluster holds exactly 256 tokens. The 256 tokens of one index of seq name one cluster at most 16 times, and each such index names some cluster exactly 16 times. block_pattern[c, b, b] = 1 and block_pattern[c, b, b2] = 0 for b2 > b.
All inputs are finite; a program needn't handle non-finite values.
Results may differ from the reference program's by a relative error of at most 0.03.
Values may be sent and summed in bfloat16 or wider, within the bound.
No kernel may reach another device: no remote copies, remote signals or barrier semaphores. Data moves between devices by JAX's collectives and lax.ppermute only.
A program may use at most 64 MiB of HBM per device.

```python
import math
import jax
import jax.numpy as jnp
from jax import lax

D = 4096
H = 32
HD = 128
BLK = 128
TOK_DEV = 256
TOKENS = 8192
CLUSTERS = 32
NB = 2
GROUP_HEADS = 4


def cluster_table(key):
    base = jax.random.fold_in(key, 5)
    key_rise, key_shift, key_order = jax.random.split(base, 3)
    even_share = TOK_DEV // CLUSTERS
    rising = jax.random.randint(key_rise, (CLUSTERS,), 0, even_share + 1)
    rising = rising.at[0].set(even_share).at[CLUSTERS - 1].set(0)
    deviation = rising - jnp.roll(rising, 1)
    shifts = jax.random.permutation(key_shift, CLUSTERS).astype(jnp.int32)
    columns = jnp.arange(CLUSTERS, dtype=jnp.int32)
    counts = even_share + deviation[(columns[None, :] - shifts[:, None]) % CLUSTERS]
    ends = jnp.cumsum(counts, axis=1)
    places = jnp.arange(TOK_DEV, dtype=jnp.int32)
    labels = jnp.sum((ends[:, None, :] <= places[None, :, None]).astype(jnp.int32), axis=2)
    orders = jax.vmap(lambda sub_key: jax.random.permutation(sub_key, TOK_DEV))(jax.random.split(key_order, CLUSTERS))
    mixed = jnp.take_along_axis(labels, orders.astype(jnp.int32), axis=1)
    return mixed


def pair_draw(key):
    base = jax.random.fold_in(key, 9)
    key_query, key_keys = jax.random.split(base, 2)
    query_vals = jnp.clip(jax.random.normal(key_query, (TOKENS, H * HD), jnp.float32), -6.0, 6.0)
    key_vals = jnp.clip(jax.random.normal(key_keys, (TOKENS, H * HD), jnp.float32), -6.0, 6.0)
    return (query_vals, key_vals)


def draw_queries(key, part):
    return pair_draw(key)[0].astype(jnp.bfloat16)


def draw_key_rows(key, part):
    return pair_draw(key)[1].astype(jnp.bfloat16)


def draw_cluster_ids(key, part):
    return cluster_table(key).reshape(TOKENS).astype(jnp.int32)


def draw_block_pattern(key, part):
    base = jax.random.fold_in(key, 13)
    coins = jax.random.randint(base, (CLUSTERS, NB, NB), 0, 2)
    row_block = jnp.arange(NB, dtype=jnp.int32)[:, None]
    col_block = jnp.arange(NB, dtype=jnp.int32)[None, :]
    return jnp.where(row_block == col_block, 1, jnp.where(row_block > col_block, coins, 0)).astype(jnp.int32)


def with_spikes(entries, stream_key, source, target, parts, factor):
    owner, partner = [(jnp.arange(entries.shape[position]) // (entries.shape[position] // parts)).reshape([-1 if axis == position else 1 for axis in range(entries.ndim)]) for position in (source, target)]
    chosen = jax.random.permutation(stream_key, parts)[partner]
    strong = (owner == chosen) | (owner == (partner + parts // 2) % parts)
    return jnp.where(strong, factor * entries, entries)


def levels(rng, extent, cuts, smallest, high):
    loudness = 1.0
    for position, blocks in cuts:
        draws = jax.random.uniform(jax.random.fold_in(jax.random.fold_in(rng, 6), position), (blocks,), jnp.float32, smallest / len(cuts), high / len(cuts))
        loudness = loudness * jnp.repeat(jnp.exp(draws), extent[position] // blocks).reshape((-1,) + (1,) * (len(extent) - 1 - position))
    return loudness


def bell_draw(own_key, shape, scale, limit, cuts=(), held_as=jnp.bfloat16):
    result = jax.random.normal(own_key, shape, jnp.float32) * scale
    if len(cuts) > 0:
        result = levels(own_key, shape, cuts, -0.22, 0.18) * result
    return jnp.clip(result, min=-limit, max=limit).astype(held_as)


def noise_with(key, shape, width, reach, shards, heavy, kind=jnp.bfloat16):
    array = width * jax.random.normal(key, shape, jnp.float32)
    if shards:
        array = array * levels(key, shape, shards, -0.22, 0.18)
    return jnp.clip(with_spikes(array, jax.random.fold_in(key, 3), *heavy), -reach, reach).astype(kind)


def setup_inputs(seed: int = 0) -> dict:
    arg_keys = jax.random.split(jax.random.key(seed), 8)
    queries = draw_queries(jax.random.fold_in(arg_keys[7], 71), 0)
    key_rows = draw_key_rows(jax.random.fold_in(arg_keys[7], 71), 0)
    value_rows = bell_draw(arg_keys[2], (TOKENS, H * HD), 1.0, 6.0, ((0, 32), (1, 8)))
    out_weight = noise_with(arg_keys[3], (H * HD, D), (H * HD) ** -0.5, 0.1875, ((0, 8), (1, 32)), (0, 1, 32, 2.75))
    grad_output = bell_draw(arg_keys[4], (TOKENS, D), 1.0, 6.0, ((0, 32), (1, 8)))
    cluster_ids = draw_cluster_ids(jax.random.fold_in(arg_keys[7], 71), 0)
    block_pattern = draw_block_pattern(jax.random.fold_in(arg_keys[7], 71), 0)
    return {"queries": queries, "key_rows": key_rows, "value_rows": value_rows, "out_weight": out_weight, "grad_output": grad_output, "cluster_ids": cluster_ids, "block_pattern": block_pattern}


def reference(queries, key_rows, value_rows, out_weight, grad_output, cluster_ids, block_pattern):
    score_scale = 1.0 / math.sqrt(HD)
    cluster_order = jnp.argsort(cluster_ids, stable=True).astype(jnp.int32).reshape(CLUSTERS, TOK_DEV)
    flat_order = cluster_order.reshape(-1)
    cluster_rank = jnp.arange(TOK_DEV, dtype=jnp.int32)
    block_of = cluster_rank // BLK
    causal = cluster_rank[None, :] <= cluster_rank[:, None]

    def allowed_of(pattern):
        return causal & (pattern[block_of][:, block_of] == 1)

    def split_heads(row_data):
        return row_data.reshape(TOK_DEV, H, HD).astype(jnp.float32)

    def rounded(values):
        return lax.optimization_barrier(values.astype(jnp.bfloat16)).astype(jnp.float32)

    def probabilities(query_heads, key_heads, allowed):
        scores = jnp.einsum('qhd,khd->hqk', query_heads, key_heads) * score_scale
        scores = jnp.where(allowed[None], scores, -jnp.inf)
        shifted = jnp.exp(scores - lax.optimization_barrier(jnp.max(scores, axis=2, keepdims=True)))
        return shifted / lax.optimization_barrier(jnp.sum(shifted, axis=2, keepdims=True))

    def forward_one(operands):
        members, pattern = operands
        probs = probabilities(split_heads(queries[members]), split_heads(key_rows[members]), allowed_of(pattern))
        mixed = jnp.einsum('hqk,khd->qhd', rounded(probs), split_heads(value_rows[members]))
        return mixed.reshape(TOK_DEV, H * HD).astype(jnp.bfloat16)
    per_cluster = lax.map(forward_one, (cluster_order, block_pattern))
    attention = jnp.zeros((TOKENS, H * HD), jnp.bfloat16).at[flat_order].set(per_cluster.reshape(TOKENS, H * HD))
    group_width = GROUP_HEADS * HD
    summed = jnp.zeros((TOKENS, D), jnp.float32)
    for group in range(H // GROUP_HEADS):
        part_cols = attention[:, group * group_width:(group + 1) * group_width]
        part_rows = out_weight[group * group_width:(group + 1) * group_width]
        summed = summed + rounded(jnp.dot(part_cols, part_rows, preferred_element_type=jnp.float32))
    layer_out = summed.astype(jnp.bfloat16)
    grad_attention = jnp.dot(grad_output, out_weight.T, preferred_element_type=jnp.float32).astype(jnp.bfloat16)

    def backward_one(operands):
        members, pattern = operands
        query_heads = split_heads(queries[members])
        key_heads = split_heads(key_rows[members])
        value_heads = split_heads(value_rows[members])
        grad_heads = split_heads(grad_attention[members])
        attn_heads = split_heads(attention[members])
        probs = probabilities(query_heads, key_heads, allowed_of(pattern))
        delta = lax.optimization_barrier(jnp.sum(grad_heads * attn_heads, axis=2)).T[:, :, None]
        dprobs = jnp.einsum('qhd,khd->hqk', grad_heads, value_heads)
        dscores = rounded(probs * (dprobs - delta))
        grad_q = jnp.einsum('hqk,khd->qhd', dscores, key_heads) * score_scale
        grad_k = jnp.einsum('hqk,qhd->khd', dscores, query_heads) * score_scale
        grad_v = jnp.einsum('hqk,qhd->khd', rounded(probs), grad_heads)
        return (grad_q.reshape(TOK_DEV, H * HD).astype(jnp.bfloat16), grad_k.reshape(TOK_DEV, H * HD).astype(jnp.bfloat16), grad_v.reshape(TOK_DEV, H * HD).astype(jnp.bfloat16))
    cluster_q, cluster_k, cluster_v = lax.map(backward_one, (cluster_order, block_pattern))

    def unsort(per_rows):
        return jnp.zeros((TOKENS, H * HD), jnp.bfloat16).at[flat_order].set(per_rows.reshape(TOKENS, H * HD))
    return (layer_out, unsort(cluster_q), unsort(cluster_k), unsort(cluster_v))
```

```python
import math

import jax
import jax.numpy as jnp
from jax import lax
from jax.sharding import PartitionSpec as P

HD = 128
BLK = 128


def select_rows(onehot, rows):
    return jnp.dot(onehot, rows, preferred_element_type=jnp.float32).astype(rows.dtype)


def select_rows_t(onehot, rows):
    return lax.dot_general(
        onehot, rows, (((0,), (0,)), ((), ())), preferred_element_type=jnp.float32
    ).astype(rows.dtype)


def on_device(queries, key_rows, value_rows, out_weight, grad_output, cluster_ids, block_pattern):
    tokens = queries.shape[0]
    width = queries.shape[1]
    head_count = width // HD
    groups = lax.axis_size("seq")
    slot_rows = 2 * tokens // groups
    slot_total = groups * slot_rows
    ranks = tokens
    owner_index = lax.axis_index("seq")
    score_scale = 1.0 / math.sqrt(HD)

    members = (cluster_ids[:, None] == jnp.arange(groups, dtype=jnp.int32)[None, :]).astype(
        jnp.int32
    )
    earlier = jnp.cumsum(members, axis=0) - members
    local_rank = jnp.sum(earlier * members, axis=1)
    send_counts = jnp.sum(members, axis=0)
    slot_index = cluster_ids * slot_rows + local_rank
    to_slot = (
        jnp.arange(slot_total, dtype=jnp.int32)[:, None] == slot_index[None, :]
    ).astype(jnp.bfloat16)

    full_weight = lax.all_gather(out_weight, "seq", axis=1, tiled=True)
    qkv = jnp.concatenate([queries, key_rows, value_rows], axis=1)
    qkv_in = lax.all_to_all(select_rows(to_slot, qkv), "seq", 0, 0, tiled=True)
    got_counts = lax.all_to_all(send_counts, "seq", 0, 0, tiled=True)

    offsets = jnp.cumsum(got_counts) - got_counts
    place = jnp.arange(slot_rows, dtype=jnp.int32)
    row_live = (place[None, :] < got_counts[:, None]).reshape(slot_total)
    rank_rows = (offsets[:, None] + place[None, :]).reshape(slot_total)
    to_rank = (
        (rank_rows[None, :] == jnp.arange(ranks, dtype=jnp.int32)[:, None]) & row_live[None, :]
    ).astype(jnp.bfloat16)
    qkv_c = select_rows(to_rank, qkv_in)
    q_c = qkv_c[:, :width].reshape(ranks, head_count, HD)
    k_c = qkv_c[:, width : 2 * width].reshape(ranks, head_count, HD)
    v_c = qkv_c[:, 2 * width :].reshape(ranks, head_count, HD)

    pattern = lax.dynamic_index_in_dim(block_pattern, owner_index, 0, keepdims=False)
    rank = jnp.arange(ranks, dtype=jnp.int32)
    blk = rank // BLK
    blk_q = blk[:, None]
    blk_k = blk[None, :]
    pat = jnp.where(
        blk_q == 0,
        jnp.where(blk_k == 0, pattern[0, 0], pattern[0, 1]),
        jnp.where(blk_k == 0, pattern[1, 0], pattern[1, 1]),
    )
    allowed = (rank[None, :] <= rank[:, None]) & (pat == 1)

    scores = (
        jnp.einsum("qhd,khd->hqk", q_c, k_c, preferred_element_type=jnp.float32) * score_scale
    )
    scores = jnp.where(allowed[None], scores, -jnp.inf)
    shifted = jnp.exp(scores - jnp.max(scores, axis=2, keepdims=True))
    probs = shifted / jnp.sum(shifted, axis=2, keepdims=True)
    probs_b = probs.astype(jnp.bfloat16)
    attn_c = jnp.einsum("hqk,khd->qhd", probs_b, v_c, preferred_element_type=jnp.float32).astype(
        jnp.bfloat16
    )

    attn_back = lax.all_to_all(
        select_rows_t(to_rank, attn_c.reshape(ranks, width)), "seq", 0, 0, tiled=True
    )
    attn_local = select_rows_t(to_slot, attn_back)
    partial_value = jnp.dot(attn_local, full_weight, preferred_element_type=jnp.float32)
    rounded_part = lax.optimization_barrier(partial_value.astype(jnp.bfloat16)).astype(jnp.float32)
    layer_out = lax.psum_scatter(
        rounded_part.astype(jnp.bfloat16), "head", scatter_dimension=1, tiled=True
    )

    grad_sum = jnp.einsum(
        "td,wd->tw",
        lax.all_gather(grad_output, "head", axis=1, tiled=True),
        full_weight,
        preferred_element_type=jnp.float32,
    )
    grad_attention = grad_sum.astype(jnp.bfloat16)
    grad_in = lax.all_to_all(select_rows(to_slot, grad_attention), "seq", 0, 0, tiled=True)
    g_c = select_rows(to_rank, grad_in).reshape(ranks, head_count, HD)

    delta = jnp.sum(g_c.astype(jnp.float32) * attn_c.astype(jnp.float32), axis=2).T[:, :, None]
    dprobs = jnp.einsum("qhd,khd->hqk", g_c, v_c, preferred_element_type=jnp.float32)
    dscores = (probs * (dprobs - delta)).astype(jnp.bfloat16)
    grad_q = (
        jnp.einsum("hqk,khd->qhd", dscores, k_c, preferred_element_type=jnp.float32) * score_scale
    ).astype(jnp.bfloat16)
    grad_k = (
        jnp.einsum("hqk,qhd->khd", dscores, q_c, preferred_element_type=jnp.float32) * score_scale
    ).astype(jnp.bfloat16)
    grad_v = jnp.einsum("hqk,qhd->khd", probs_b, g_c, preferred_element_type=jnp.float32).astype(
        jnp.bfloat16
    )
    grads_c = jnp.concatenate(
        [
            grad_q.reshape(ranks, width),
            grad_k.reshape(ranks, width),
            grad_v.reshape(ranks, width),
        ],
        axis=1,
    )
    grads_back = lax.all_to_all(select_rows_t(to_rank, grads_c), "seq", 0, 0, tiled=True)
    grads_local = select_rows_t(to_slot, grads_back)
    return (
        layer_out,
        grads_local[:, :width],
        grads_local[:, width : 2 * width],
        grads_local[:, 2 * width :],
    )


def solution(mesh):
    in_specs = (
        P("seq", "head"),
        P("seq", "head"),
        P("seq", "head"),
        P("head", "seq"),
        P("seq", "head"),
        P("seq"),
        P(),
    )
    out_specs = (P("seq", "head"), P("seq", "head"), P("seq", "head"), P("seq", "head"))
    return jax.shard_map(
        on_device, mesh=mesh, in_specs=in_specs, out_specs=out_specs, check_vma=False
    )
```

```python
import math

import jax
import jax.numpy as jnp
from jax import lax
from jax.sharding import PartitionSpec as P

HD = 128
BLK = 128


def select_rows(onehot, rows):
    return jnp.dot(onehot, rows, preferred_element_type=jnp.float32).astype(rows.dtype)


def select_rows_t(onehot, rows):
    return lax.dot_general(
        onehot, rows, (((0,), (0,)), ((), ())), preferred_element_type=jnp.float32
    ).astype(rows.dtype)


def on_device(queries, key_rows, value_rows, out_weight, grad_output, cluster_ids, block_pattern):
    tokens = queries.shape[0]
    width = queries.shape[1]
    head_count = width // HD
    groups = lax.axis_size("seq")
    slot_rows = 2 * tokens // groups
    slot_total = groups * slot_rows
    ranks = tokens
    owner_index = lax.axis_index("seq")
    score_scale = 1.0 / math.sqrt(HD)

    members = (cluster_ids[:, None] == jnp.arange(groups, dtype=jnp.int32)[None, :]).astype(
        jnp.int32
    )
    earlier = jnp.cumsum(members, axis=0) - members
    local_rank = jnp.sum(earlier * members, axis=1)
    send_counts = jnp.sum(members, axis=0)
    slot_index = cluster_ids * slot_rows + local_rank
    to_slot = (
        jnp.arange(slot_total, dtype=jnp.int32)[:, None] == slot_index[None, :]
    ).astype(jnp.bfloat16)

    cols = out_weight.shape[1]
    heads_n = lax.axis_size("head")
    w_blocks = lax.all_gather(out_weight, "seq", axis=0, tiled=False)
    w_grouped = w_blocks.reshape(heads_n, groups // heads_n, out_weight.shape[0], cols)
    qkv = jnp.concatenate([queries, key_rows, value_rows], axis=1)
    qkv_in = lax.all_to_all(select_rows(to_slot, qkv), "seq", 0, 0, tiled=True)
    got_counts = lax.all_to_all(send_counts, "seq", 0, 0, tiled=True)

    offsets = jnp.cumsum(got_counts) - got_counts
    place = jnp.arange(slot_rows, dtype=jnp.int32)
    row_live = (place[None, :] < got_counts[:, None]).reshape(slot_total)
    rank_rows = (offsets[:, None] + place[None, :]).reshape(slot_total)
    to_rank = (
        (rank_rows[None, :] == jnp.arange(ranks, dtype=jnp.int32)[:, None]) & row_live[None, :]
    ).astype(jnp.bfloat16)
    qkv_c = select_rows(to_rank, qkv_in)
    q_c = qkv_c[:, :width].reshape(ranks, head_count, HD)
    k_c = qkv_c[:, width : 2 * width].reshape(ranks, head_count, HD)
    v_c = qkv_c[:, 2 * width :].reshape(ranks, head_count, HD)

    pattern = lax.dynamic_index_in_dim(block_pattern, owner_index, 0, keepdims=False)
    rank = jnp.arange(ranks, dtype=jnp.int32)
    blk = rank // BLK
    blk_q = blk[:, None]
    blk_k = blk[None, :]
    pat = jnp.where(
        blk_q == 0,
        jnp.where(blk_k == 0, pattern[0, 0], pattern[0, 1]),
        jnp.where(blk_k == 0, pattern[1, 0], pattern[1, 1]),
    )
    allowed = (rank[None, :] <= rank[:, None]) & (pat == 1)

    scores = (
        jnp.einsum("qhd,khd->hqk", q_c, k_c, preferred_element_type=jnp.float32) * score_scale
    )
    scores = jnp.where(allowed[None], scores, -jnp.inf)
    shifted = jnp.exp(scores - jnp.max(scores, axis=2, keepdims=True))
    probs = shifted / jnp.sum(shifted, axis=2, keepdims=True)
    probs_b = probs.astype(jnp.bfloat16)
    attn_c = jnp.einsum("hqk,khd->qhd", probs_b, v_c, preferred_element_type=jnp.float32).astype(
        jnp.bfloat16
    )

    attn_back = lax.all_to_all(
        select_rows_t(to_rank, attn_c.reshape(ranks, width)), "seq", 0, 0, tiled=True
    )
    attn_local = select_rows_t(to_slot, attn_back)
    partial_value = jnp.einsum(
        "tr,kjrc->ktjc", attn_local, w_grouped, preferred_element_type=jnp.float32
    ).reshape(heads_n, tokens, -1)
    rounded_part = lax.optimization_barrier(partial_value.astype(jnp.bfloat16)).astype(jnp.float32)
    layer_out = lax.psum_scatter(
        rounded_part.astype(jnp.bfloat16), "head", scatter_dimension=0, tiled=False
    )

    grad_blocks = lax.all_gather(grad_output, "head", axis=0, tiled=False).reshape(
        heads_n, tokens, groups // heads_n, cols
    )
    grad_sum = jnp.einsum(
        "ktjc,kjwc->tw", grad_blocks, w_grouped, preferred_element_type=jnp.float32
    )
    grad_attention = grad_sum.astype(jnp.bfloat16)
    grad_in = lax.all_to_all(select_rows(to_slot, grad_attention), "seq", 0, 0, tiled=True)
    g_c = select_rows(to_rank, grad_in).reshape(ranks, head_count, HD)

    delta = jnp.sum(g_c.astype(jnp.float32) * attn_c.astype(jnp.float32), axis=2).T[:, :, None]
    dprobs = jnp.einsum("qhd,khd->hqk", g_c, v_c, preferred_element_type=jnp.float32)
    dscores = (probs * (dprobs - delta)).astype(jnp.bfloat16)
    grad_q = (
        jnp.einsum("hqk,khd->qhd", dscores, k_c, preferred_element_type=jnp.float32) * score_scale
    ).astype(jnp.bfloat16)
    grad_k = (
        jnp.einsum("hqk,qhd->khd", dscores, q_c, preferred_element_type=jnp.float32) * score_scale
    ).astype(jnp.bfloat16)
    grad_v = jnp.einsum("hqk,qhd->khd", probs_b, g_c, preferred_element_type=jnp.float32).astype(
        jnp.bfloat16
    )
    grads_c = jnp.concatenate(
        [
            grad_q.reshape(ranks, width),
            grad_k.reshape(ranks, width),
            grad_v.reshape(ranks, width),
        ],
        axis=1,
    )
    grads_back = lax.all_to_all(select_rows_t(to_rank, grads_c), "seq", 0, 0, tiled=True)
    grads_local = select_rows_t(to_slot, grads_back)
    return (
        layer_out,
        grads_local[:, :width],
        grads_local[:, width : 2 * width],
        grads_local[:, 2 * width :],
    )


def solution(mesh):
    in_specs = (
        P("seq", "head"),
        P("seq", "head"),
        P("seq", "head"),
        P("head", "seq"),
        P("seq", "head"),
        P("seq"),
        P(),
    )
    out_specs = (P("seq", "head"), P("seq", "head"), P("seq", "head"), P("seq", "head"))
    return jax.shard_map(
        on_device, mesh=mesh, in_specs=in_specs, out_specs=out_specs, check_vma=False
    )
```

```python
import math

import jax
import jax.numpy as jnp
from jax import lax
from jax.sharding import PartitionSpec as P

HD = 128
BLK = 128


def select_rows(onehot, rows):
    return jnp.dot(onehot, rows, preferred_element_type=jnp.float32).astype(rows.dtype)


def select_rows_t(onehot, rows):
    return lax.dot_general(
        onehot, rows, (((0,), (0,)), ((), ())), preferred_element_type=jnp.float32
    ).astype(rows.dtype)


def ring_gather_cols(block, axis_name, ny, nz):
    index = lax.axis_index(axis_name)
    y = index % ny
    z = index // ny
    n = ny * nz
    cols = block.shape[1]

    def perm(dy, dz):
        return [(i, ((i // ny + dz) % nz) * ny + (i % ny + dy) % ny) for i in range(n)]

    def ring(piece, pos, count, step_perm, width, total):
        out = jnp.zeros((piece.shape[0], total), piece.dtype)
        out = lax.dynamic_update_slice(out, piece, (0, pos * width))
        fwd = piece
        bwd = piece
        for step in range(1, count // 2 + 1):
            fwd = lax.ppermute(fwd, axis_name, step_perm(1))
            out = lax.dynamic_update_slice(out, fwd, (0, ((pos - step) % count) * width))
            if count - step != step:
                bwd = lax.ppermute(bwd, axis_name, step_perm(-1))
                out = lax.dynamic_update_slice(out, bwd, (0, ((pos + step) % count) * width))
        return out

    row = ring(block, y, ny, lambda d: perm(d, 0), cols, ny * cols)
    return ring(row, z, nz, lambda d: perm(0, d), ny * cols, n * cols)


def on_device(queries, key_rows, value_rows, out_weight, grad_output, cluster_ids, block_pattern):
    tokens = queries.shape[0]
    width = queries.shape[1]
    head_count = width // HD
    groups = lax.axis_size("seq")
    slot_rows = 2 * tokens // groups
    slot_total = groups * slot_rows
    ranks = tokens
    owner_index = lax.axis_index("seq")
    score_scale = 1.0 / math.sqrt(HD)

    members = (cluster_ids[:, None] == jnp.arange(groups, dtype=jnp.int32)[None, :]).astype(
        jnp.int32
    )
    earlier = jnp.cumsum(members, axis=0) - members
    local_rank = jnp.sum(earlier * members, axis=1)
    send_counts = jnp.sum(members, axis=0)
    slot_index = cluster_ids * slot_rows + local_rank
    to_slot = (
        jnp.arange(slot_total, dtype=jnp.int32)[:, None] == slot_index[None, :]
    ).astype(jnp.bfloat16)

    ring_y = 4 if groups % 4 == 0 else 1
    full_weight = ring_gather_cols(out_weight, "seq", ring_y, groups // ring_y)
    qkv = jnp.concatenate([queries, key_rows, value_rows], axis=1)
    qkv_in = lax.all_to_all(select_rows(to_slot, qkv), "seq", 0, 0, tiled=True)
    got_counts = lax.all_to_all(send_counts, "seq", 0, 0, tiled=True)

    offsets = jnp.cumsum(got_counts) - got_counts
    place = jnp.arange(slot_rows, dtype=jnp.int32)
    row_live = (place[None, :] < got_counts[:, None]).reshape(slot_total)
    rank_rows = (offsets[:, None] + place[None, :]).reshape(slot_total)
    to_rank = (
        (rank_rows[None, :] == jnp.arange(ranks, dtype=jnp.int32)[:, None]) & row_live[None, :]
    ).astype(jnp.bfloat16)
    qkv_c = select_rows(to_rank, qkv_in)
    q_c = qkv_c[:, :width].reshape(ranks, head_count, HD)
    k_c = qkv_c[:, width : 2 * width].reshape(ranks, head_count, HD)
    v_c = qkv_c[:, 2 * width :].reshape(ranks, head_count, HD)

    pattern = lax.dynamic_index_in_dim(block_pattern, owner_index, 0, keepdims=False)
    rank = jnp.arange(ranks, dtype=jnp.int32)
    blk = rank // BLK
    blk_q = blk[:, None]
    blk_k = blk[None, :]
    pat = jnp.where(
        blk_q == 0,
        jnp.where(blk_k == 0, pattern[0, 0], pattern[0, 1]),
        jnp.where(blk_k == 0, pattern[1, 0], pattern[1, 1]),
    )
    allowed = (rank[None, :] <= rank[:, None]) & (pat == 1)

    scores = (
        jnp.einsum("qhd,khd->hqk", q_c, k_c, preferred_element_type=jnp.float32) * score_scale
    )
    scores = jnp.where(allowed[None], scores, -jnp.inf)
    shifted = jnp.exp(scores - jnp.max(scores, axis=2, keepdims=True))
    probs = shifted / jnp.sum(shifted, axis=2, keepdims=True)
    probs_b = probs.astype(jnp.bfloat16)
    attn_c = jnp.einsum("hqk,khd->qhd", probs_b, v_c, preferred_element_type=jnp.float32).astype(
        jnp.bfloat16
    )

    attn_back = lax.all_to_all(
        select_rows_t(to_rank, attn_c.reshape(ranks, width)), "seq", 0, 0, tiled=True
    )
    attn_back, full_weight = lax.optimization_barrier((attn_back, full_weight))
    attn_local = select_rows_t(to_slot, attn_back)
    partial_value = jnp.dot(attn_local, full_weight, preferred_element_type=jnp.float32)
    rounded_part = lax.optimization_barrier(partial_value.astype(jnp.bfloat16)).astype(jnp.float32)
    layer_out = lax.psum_scatter(
        rounded_part.astype(jnp.bfloat16), "head", scatter_dimension=1, tiled=True
    )

    grad_sum = jnp.einsum(
        "td,wd->tw",
        lax.all_gather(grad_output, "head", axis=1, tiled=True),
        full_weight,
        preferred_element_type=jnp.float32,
    )
    grad_attention = grad_sum.astype(jnp.bfloat16)
    grad_in = lax.all_to_all(select_rows(to_slot, grad_attention), "seq", 0, 0, tiled=True)
    g_c = select_rows(to_rank, grad_in).reshape(ranks, head_count, HD)

    delta = jnp.sum(g_c.astype(jnp.float32) * attn_c.astype(jnp.float32), axis=2).T[:, :, None]
    dprobs = jnp.einsum("qhd,khd->hqk", g_c, v_c, preferred_element_type=jnp.float32)
    dscores = (probs * (dprobs - delta)).astype(jnp.bfloat16)
    grad_q = (
        jnp.einsum("hqk,khd->qhd", dscores, k_c, preferred_element_type=jnp.float32) * score_scale
    ).astype(jnp.bfloat16)
    grad_k = (
        jnp.einsum("hqk,qhd->khd", dscores, q_c, preferred_element_type=jnp.float32) * score_scale
    ).astype(jnp.bfloat16)
    grad_v = jnp.einsum("hqk,qhd->khd", probs_b, g_c, preferred_element_type=jnp.float32).astype(
        jnp.bfloat16
    )
    grads_c = jnp.concatenate(
        [
            grad_q.reshape(ranks, width),
            grad_k.reshape(ranks, width),
            grad_v.reshape(ranks, width),
        ],
        axis=1,
    )
    grads_back = lax.all_to_all(select_rows_t(to_rank, grads_c), "seq", 0, 0, tiled=True)
    grads_local = select_rows_t(to_slot, grads_back)
    return (
        layer_out,
        grads_local[:, :width],
        grads_local[:, width : 2 * width],
        grads_local[:, 2 * width :],
    )


def solution(mesh):
    in_specs = (
        P("seq", "head"),
        P("seq", "head"),
        P("seq", "head"),
        P("head", "seq"),
        P("seq", "head"),
        P("seq"),
        P(),
    )
    out_specs = (P("seq", "head"), P("seq", "head"), P("seq", "head"), P("seq", "head"))
    return jax.shard_map(
        on_device, mesh=mesh, in_specs=in_specs, out_specs=out_specs, check_vma=False
    )
```

```python
import math

import jax
import jax.numpy as jnp
from jax import lax
from jax.sharding import PartitionSpec as P

HD = 128
BLK = 128


def select_rows(onehot, rows):
    return jnp.dot(onehot, rows, preferred_element_type=jnp.float32).astype(rows.dtype)


def select_rows_t(onehot, rows):
    return lax.dot_general(
        onehot, rows, (((0,), (0,)), ((), ())), preferred_element_type=jnp.float32
    ).astype(rows.dtype)


def ring_gather_cols(block, axis_name, ny, nz):
    index = lax.axis_index(axis_name)
    y = index % ny
    z = index // ny
    n = ny * nz
    cols = block.shape[1]

    def perm(dy, dz):
        return [(i, ((i // ny + dz) % nz) * ny + (i % ny + dy) % ny) for i in range(n)]

    def ring(piece, pos, count, step_perm, width, total):
        out = jnp.zeros((piece.shape[0], total), piece.dtype)
        out = lax.dynamic_update_slice(out, piece, (0, pos * width))
        fwd = piece
        bwd = piece
        for step in range(1, count // 2 + 1):
            fwd = lax.ppermute(fwd, axis_name, step_perm(1))
            out = lax.dynamic_update_slice(out, fwd, (0, ((pos - step) % count) * width))
            if count - step != step:
                bwd = lax.ppermute(bwd, axis_name, step_perm(-1))
                out = lax.dynamic_update_slice(out, bwd, (0, ((pos + step) % count) * width))
        return out

    row = ring(block, y, ny, lambda d: perm(d, 0), cols, ny * cols)
    return ring(row, z, nz, lambda d: perm(0, d), ny * cols, n * cols)


def on_device(queries, key_rows, value_rows, out_weight, grad_output, cluster_ids, block_pattern):
    tokens = queries.shape[0]
    width = queries.shape[1]
    head_count = width // HD
    groups = lax.axis_size("seq")
    slot_rows = 2 * tokens // groups
    slot_total = groups * slot_rows
    ranks = tokens
    owner_index = lax.axis_index("seq")
    score_scale = 1.0 / math.sqrt(HD)

    members = (cluster_ids[:, None] == jnp.arange(groups, dtype=jnp.int32)[None, :]).astype(
        jnp.int32
    )
    earlier = jnp.cumsum(members, axis=0) - members
    local_rank = jnp.sum(earlier * members, axis=1)
    send_counts = jnp.sum(members, axis=0)
    slot_index = cluster_ids * slot_rows + local_rank
    to_slot = (
        jnp.arange(slot_total, dtype=jnp.int32)[:, None] == slot_index[None, :]
    ).astype(jnp.bfloat16)

    ring_y = 4 if groups % 4 == 0 else 1
    full_weight = ring_gather_cols(out_weight, "seq", ring_y, groups // ring_y)
    qkv = jnp.concatenate([queries, key_rows, value_rows], axis=1)
    qkv_in = lax.all_to_all(select_rows(to_slot, qkv), "seq", 0, 0, tiled=True)
    got_counts = lax.all_to_all(send_counts, "seq", 0, 0, tiled=True)

    offsets = jnp.cumsum(got_counts) - got_counts
    place = jnp.arange(slot_rows, dtype=jnp.int32)
    row_live = (place[None, :] < got_counts[:, None]).reshape(slot_total)
    rank_rows = (offsets[:, None] + place[None, :]).reshape(slot_total)
    to_rank = (
        (rank_rows[None, :] == jnp.arange(ranks, dtype=jnp.int32)[:, None]) & row_live[None, :]
    ).astype(jnp.bfloat16)
    qkv_c = select_rows(to_rank, qkv_in)
    q_c = qkv_c[:, :width].reshape(ranks, head_count, HD)
    k_c = qkv_c[:, width : 2 * width].reshape(ranks, head_count, HD)
    v_c = qkv_c[:, 2 * width :].reshape(ranks, head_count, HD)

    pattern = lax.dynamic_index_in_dim(block_pattern, owner_index, 0, keepdims=False)
    rank = jnp.arange(ranks, dtype=jnp.int32)
    blk = rank // BLK
    blk_q = blk[:, None]
    blk_k = blk[None, :]
    pat = jnp.where(
        blk_q == 0,
        jnp.where(blk_k == 0, pattern[0, 0], pattern[0, 1]),
        jnp.where(blk_k == 0, pattern[1, 0], pattern[1, 1]),
    )
    allowed = (rank[None, :] <= rank[:, None]) & (pat == 1)

    scores = (
        jnp.einsum("qhd,khd->hqk", q_c, k_c, preferred_element_type=jnp.float32) * score_scale
    )
    scores = jnp.where(allowed[None], scores, -jnp.inf)
    shifted = jnp.exp(scores - jnp.max(scores, axis=2, keepdims=True))
    probs = shifted / jnp.sum(shifted, axis=2, keepdims=True)
    probs_b = probs.astype(jnp.bfloat16)
    attn_c = jnp.einsum("hqk,khd->qhd", probs_b, v_c, preferred_element_type=jnp.float32).astype(
        jnp.bfloat16
    )

    attn_back = lax.all_to_all(
        select_rows_t(to_rank, attn_c.reshape(ranks, width)), "seq", 0, 0, tiled=True
    )
    attn_back, full_weight = lax.optimization_barrier((attn_back, full_weight))
    attn_local = select_rows_t(to_slot, attn_back)
    partial_value = jnp.dot(attn_local, full_weight, preferred_element_type=jnp.float32)
    rounded_part = lax.optimization_barrier(partial_value.astype(jnp.bfloat16)).astype(jnp.float32)
    layer_out = lax.psum_scatter(
        rounded_part.astype(jnp.bfloat16), "head", scatter_dimension=1, tiled=True
    )

    grad_sum = jnp.einsum(
        "td,wd->tw",
        lax.all_gather(grad_output, "head", axis=1, tiled=True),
        full_weight,
        preferred_element_type=jnp.float32,
    )
    grad_attention = grad_sum.astype(jnp.bfloat16)
    grad_in = lax.all_to_all(select_rows(to_slot, grad_attention), "seq", 0, 0, tiled=True)
    g_c = select_rows(to_rank, grad_in).reshape(ranks, head_count, HD)

    delta = jnp.sum(g_c.astype(jnp.float32) * attn_c.astype(jnp.float32), axis=2).T[:, :, None]
    dprobs = jnp.einsum("qhd,khd->hqk", g_c, v_c, preferred_element_type=jnp.float32)
    dscores = (probs * (dprobs - delta)).astype(jnp.bfloat16)
    grad_q = (
        jnp.einsum("hqk,khd->qhd", dscores, k_c, preferred_element_type=jnp.float32) * score_scale
    ).astype(jnp.bfloat16)
    grad_k = (
        jnp.einsum("hqk,qhd->khd", dscores, q_c, preferred_element_type=jnp.float32) * score_scale
    ).astype(jnp.bfloat16)
    grad_v = jnp.einsum("hqk,qhd->khd", probs_b, g_c, preferred_element_type=jnp.float32).astype(
        jnp.bfloat16
    )
    back_v = lax.all_to_all(
        select_rows_t(to_rank, grad_v.reshape(ranks, width)), "seq", 0, 0, tiled=True
    )
    grads_qk = jnp.concatenate([grad_q.reshape(ranks, width), grad_k.reshape(ranks, width)], axis=1)
    back_qk = lax.all_to_all(select_rows_t(to_rank, grads_qk), "seq", 0, 0, tiled=True)
    local_qk = select_rows_t(to_slot, back_qk)
    return (
        layer_out,
        local_qk[:, :width],
        local_qk[:, width:],
        select_rows_t(to_slot, back_v),
    )


def solution(mesh):
    in_specs = (
        P("seq", "head"),
        P("seq", "head"),
        P("seq", "head"),
        P("head", "seq"),
        P("seq", "head"),
        P("seq"),
        P(),
    )
    out_specs = (P("seq", "head"), P("seq", "head"), P("seq", "head"), P("seq", "head"))
    return jax.shard_map(
        on_device, mesh=mesh, in_specs=in_specs, out_specs=out_specs, check_vma=False
    )
```

```python
import math

import jax
import jax.numpy as jnp
from jax import lax
from jax.sharding import PartitionSpec as P

HD = 128
BLK = 128


def select_rows(onehot, rows):
    return jnp.dot(onehot, rows, preferred_element_type=jnp.float32).astype(rows.dtype)


def select_rows_t(onehot, rows):
    return lax.dot_general(
        onehot, rows, (((0,), (0,)), ((), ())), preferred_element_type=jnp.float32
    ).astype(rows.dtype)


def ring_gather_cols(block, axis_name, ny, nz):
    index = lax.axis_index(axis_name)
    y = index % ny
    z = index // ny
    n = ny * nz
    cols = block.shape[1]

    def perm(dy, dz):
        return [(i, ((i // ny + dz) % nz) * ny + (i % ny + dy) % ny) for i in range(n)]

    def ring(piece, pos, count, step_perm, width, total):
        out = jnp.zeros((piece.shape[0], total), piece.dtype)
        out = lax.dynamic_update_slice(out, piece, (0, pos * width))
        fwd = piece
        bwd = piece
        for step in range(1, count // 2 + 1):
            fwd = lax.ppermute(fwd, axis_name, step_perm(1))
            out = lax.dynamic_update_slice(out, fwd, (0, ((pos - step) % count) * width))
            if count - step != step:
                bwd = lax.ppermute(bwd, axis_name, step_perm(-1))
                out = lax.dynamic_update_slice(out, bwd, (0, ((pos + step) % count) * width))
        return out

    row = ring(block, y, ny, lambda d: perm(d, 0), cols, ny * cols)
    return ring(row, z, nz, lambda d: perm(0, d), ny * cols, n * cols), row


def on_device(queries, key_rows, value_rows, out_weight, grad_output, cluster_ids, block_pattern):
    tokens = queries.shape[0]
    width = queries.shape[1]
    head_count = width // HD
    groups = lax.axis_size("seq")
    slot_rows = 2 * tokens // groups
    slot_total = groups * slot_rows
    ranks = tokens
    owner_index = lax.axis_index("seq")
    score_scale = 1.0 / math.sqrt(HD)

    members = (cluster_ids[:, None] == jnp.arange(groups, dtype=jnp.int32)[None, :]).astype(
        jnp.int32
    )
    earlier = jnp.cumsum(members, axis=0) - members
    local_rank = jnp.sum(earlier * members, axis=1)
    send_counts = jnp.sum(members, axis=0)
    slot_index = cluster_ids * slot_rows + local_rank
    to_slot = (
        jnp.arange(slot_total, dtype=jnp.int32)[:, None] == slot_index[None, :]
    ).astype(jnp.bfloat16)

    ring_y = 4 if groups % 4 == 0 else 1
    full_weight, weight_row = ring_gather_cols(out_weight, "seq", ring_y, groups // ring_y)
    qkv = jnp.concatenate([queries, key_rows, value_rows], axis=1)
    qkv_slots, _ = lax.optimization_barrier((select_rows(to_slot, qkv), weight_row))
    qkv_in = lax.all_to_all(qkv_slots, "seq", 0, 0, tiled=True)
    got_counts = lax.all_to_all(send_counts, "seq", 0, 0, tiled=True)

    offsets = jnp.cumsum(got_counts) - got_counts
    place = jnp.arange(slot_rows, dtype=jnp.int32)
    row_live = (place[None, :] < got_counts[:, None]).reshape(slot_total)
    rank_rows = (offsets[:, None] + place[None, :]).reshape(slot_total)
    to_rank = (
        (rank_rows[None, :] == jnp.arange(ranks, dtype=jnp.int32)[:, None]) & row_live[None, :]
    ).astype(jnp.bfloat16)
    qkv_c = select_rows(to_rank, qkv_in)
    q_c = qkv_c[:, :width].reshape(ranks, head_count, HD)
    k_c = qkv_c[:, width : 2 * width].reshape(ranks, head_count, HD)
    v_c = qkv_c[:, 2 * width :].reshape(ranks, head_count, HD)

    pattern = lax.dynamic_index_in_dim(block_pattern, owner_index, 0, keepdims=False)
    rank = jnp.arange(ranks, dtype=jnp.int32)
    blk = rank // BLK
    blk_q = blk[:, None]
    blk_k = blk[None, :]
    pat = jnp.where(
        blk_q == 0,
        jnp.where(blk_k == 0, pattern[0, 0], pattern[0, 1]),
        jnp.where(blk_k == 0, pattern[1, 0], pattern[1, 1]),
    )
    allowed = (rank[None, :] <= rank[:, None]) & (pat == 1)

    scores = (
        jnp.einsum("qhd,khd->hqk", q_c, k_c, preferred_element_type=jnp.float32) * score_scale
    )
    scores = jnp.where(allowed[None], scores, -jnp.inf)
    shifted = jnp.exp(scores - jnp.max(scores, axis=2, keepdims=True))
    probs = shifted / jnp.sum(shifted, axis=2, keepdims=True)
    probs_b = probs.astype(jnp.bfloat16)
    attn_c = jnp.einsum("hqk,khd->qhd", probs_b, v_c, preferred_element_type=jnp.float32).astype(
        jnp.bfloat16
    )

    attn_back = lax.all_to_all(
        select_rows_t(to_rank, attn_c.reshape(ranks, width)), "seq", 0, 0, tiled=True
    )
    attn_back, full_weight = lax.optimization_barrier((attn_back, full_weight))
    attn_local = select_rows_t(to_slot, attn_back)
    partial_value = jnp.dot(attn_local, full_weight, preferred_element_type=jnp.float32)
    rounded_part = lax.optimization_barrier(partial_value.astype(jnp.bfloat16)).astype(jnp.float32)
    layer_out = lax.psum_scatter(
        rounded_part.astype(jnp.bfloat16), "head", scatter_dimension=1, tiled=True
    )

    grad_sum = jnp.einsum(
        "td,wd->tw",
        lax.all_gather(grad_output, "head", axis=1, tiled=True),
        full_weight,
        preferred_element_type=jnp.float32,
    )
    grad_attention = grad_sum.astype(jnp.bfloat16)
    grad_in = lax.all_to_all(select_rows(to_slot, grad_attention), "seq", 0, 0, tiled=True)
    g_c = select_rows(to_rank, grad_in).reshape(ranks, head_count, HD)

    delta = jnp.sum(g_c.astype(jnp.float32) * attn_c.astype(jnp.float32), axis=2).T[:, :, None]
    dprobs = jnp.einsum("qhd,khd->hqk", g_c, v_c, preferred_element_type=jnp.float32)
    dscores = (probs * (dprobs - delta)).astype(jnp.bfloat16)
    grad_q = (
        jnp.einsum("hqk,khd->qhd", dscores, k_c, preferred_element_type=jnp.float32) * score_scale
    ).astype(jnp.bfloat16)
    grad_k = (
        jnp.einsum("hqk,qhd->khd", dscores, q_c, preferred_element_type=jnp.float32) * score_scale
    ).astype(jnp.bfloat16)
    grad_v = jnp.einsum("hqk,qhd->khd", probs_b, g_c, preferred_element_type=jnp.float32).astype(
        jnp.bfloat16
    )
    grads_c = jnp.concatenate(
        [
            grad_q.reshape(ranks, width),
            grad_k.reshape(ranks, width),
            grad_v.reshape(ranks, width),
        ],
        axis=1,
    )
    grads_back = lax.all_to_all(select_rows_t(to_rank, grads_c), "seq", 0, 0, tiled=True)
    grads_local = select_rows_t(to_slot, grads_back)
    return (
        layer_out,
        grads_local[:, :width],
        grads_local[:, width : 2 * width],
        grads_local[:, 2 * width :],
    )


def solution(mesh):
    in_specs = (
        P("seq", "head"),
        P("seq", "head"),
        P("seq", "head"),
        P("head", "seq"),
        P("seq", "head"),
        P("seq"),
        P(),
    )
    out_specs = (P("seq", "head"), P("seq", "head"), P("seq", "head"), P("seq", "head"))
    return jax.shard_map(
        on_device, mesh=mesh, in_specs=in_specs, out_specs=out_specs, check_vma=False
    )
```

```python
import math

import jax
import jax.numpy as jnp
from jax import lax
from jax.sharding import PartitionSpec as P

HD = 128
BLK = 128


def select_rows(onehot, rows):
    return jnp.dot(onehot, rows, preferred_element_type=jnp.float32).astype(rows.dtype)


def select_rows_t(onehot, rows):
    return lax.dot_general(
        onehot, rows, (((0,), (0,)), ((), ())), preferred_element_type=jnp.float32
    ).astype(rows.dtype)


def ring_gather_cols(block, axis_name, ny, nz):
    index = lax.axis_index(axis_name)
    y = index % ny
    z = index // ny
    n = ny * nz
    cols = block.shape[1]

    def perm(dy, dz):
        return [(i, ((i // ny + dz) % nz) * ny + (i % ny + dy) % ny) for i in range(n)]

    def ring(piece, pos, count, step_perm, width, total):
        out = jnp.zeros((piece.shape[0], total), piece.dtype)
        out = lax.dynamic_update_slice(out, piece, (0, pos * width))
        fwd = piece
        bwd = piece
        for step in range(1, count // 2 + 1):
            fwd = lax.ppermute(fwd, axis_name, step_perm(1))
            out = lax.dynamic_update_slice(out, fwd, (0, ((pos - step) % count) * width))
            if count - step != step:
                bwd = lax.ppermute(bwd, axis_name, step_perm(-1))
                out = lax.dynamic_update_slice(out, bwd, (0, ((pos + step) % count) * width))
        return out

    row = ring(block, y, ny, lambda d: perm(d, 0), cols, ny * cols)
    return ring(row, z, nz, lambda d: perm(0, d), ny * cols, n * cols)


def on_device(queries, key_rows, value_rows, out_weight, grad_output, cluster_ids, block_pattern):
    tokens = queries.shape[0]
    width = queries.shape[1]
    head_count = width // HD
    groups = lax.axis_size("seq")
    slot_rows = 2 * tokens // groups
    slot_total = groups * slot_rows
    ranks = tokens
    owner_index = lax.axis_index("seq")
    score_scale = 1.0 / math.sqrt(HD)

    members = (cluster_ids[:, None] == jnp.arange(groups, dtype=jnp.int32)[None, :]).astype(
        jnp.int32
    )
    earlier = jnp.cumsum(members, axis=0) - members
    local_rank = jnp.sum(earlier * members, axis=1)
    slot_index = cluster_ids * slot_rows + local_rank
    to_slot = (
        jnp.arange(slot_total, dtype=jnp.int32)[:, None] == slot_index[None, :]
    ).astype(jnp.bfloat16)

    ring_y = 4 if groups % 4 == 0 else 1
    full_weight = ring_gather_cols(out_weight, "seq", ring_y, groups // ring_y)
    live_flag = jnp.ones((tokens, HD), queries.dtype)
    qkv = jnp.concatenate([queries, key_rows, value_rows, live_flag], axis=1)
    qkv_in = lax.all_to_all(select_rows(to_slot, qkv), "seq", 0, 0, tiled=True)

    row_live = qkv_in[:, 3 * width] > 0.5
    got_counts = jnp.sum(row_live.reshape(groups, slot_rows).astype(jnp.int32), axis=1)
    offsets = jnp.cumsum(got_counts) - got_counts
    place = jnp.arange(slot_rows, dtype=jnp.int32)
    rank_rows = (offsets[:, None] + place[None, :]).reshape(slot_total)
    to_rank = (
        (rank_rows[None, :] == jnp.arange(ranks, dtype=jnp.int32)[:, None]) & row_live[None, :]
    ).astype(jnp.bfloat16)
    qkv_c = select_rows(to_rank, qkv_in)
    q_c = qkv_c[:, :width].reshape(ranks, head_count, HD)
    k_c = qkv_c[:, width : 2 * width].reshape(ranks, head_count, HD)
    v_c = qkv_c[:, 2 * width : 3 * width].reshape(ranks, head_count, HD)

    pattern = lax.dynamic_index_in_dim(block_pattern, owner_index, 0, keepdims=False)
    rank = jnp.arange(ranks, dtype=jnp.int32)
    blk = rank // BLK
    blk_q = blk[:, None]
    blk_k = blk[None, :]
    pat = jnp.where(
        blk_q == 0,
        jnp.where(blk_k == 0, pattern[0, 0], pattern[0, 1]),
        jnp.where(blk_k == 0, pattern[1, 0], pattern[1, 1]),
    )
    allowed = (rank[None, :] <= rank[:, None]) & (pat == 1)

    scores = (
        jnp.einsum("qhd,khd->hqk", q_c, k_c, preferred_element_type=jnp.float32) * score_scale
    )
    scores = jnp.where(allowed[None], scores, -jnp.inf)
    shifted = jnp.exp(scores - jnp.max(scores, axis=2, keepdims=True))
    probs = shifted / jnp.sum(shifted, axis=2, keepdims=True)
    probs_b = probs.astype(jnp.bfloat16)
    attn_c = jnp.einsum("hqk,khd->qhd", probs_b, v_c, preferred_element_type=jnp.float32).astype(
        jnp.bfloat16
    )

    attn_back = lax.all_to_all(
        select_rows_t(to_rank, attn_c.reshape(ranks, width)), "seq", 0, 0, tiled=True
    )
    attn_back, full_weight = lax.optimization_barrier((attn_back, full_weight))
    attn_local = select_rows_t(to_slot, attn_back)
    partial_value = jnp.dot(attn_local, full_weight, preferred_element_type=jnp.float32)
    rounded_part = lax.optimization_barrier(partial_value.astype(jnp.bfloat16)).astype(jnp.float32)
    layer_out = lax.psum_scatter(
        rounded_part.astype(jnp.bfloat16), "head", scatter_dimension=1, tiled=True
    )

    grad_sum = jnp.einsum(
        "td,wd->tw",
        lax.all_gather(grad_output, "head", axis=1, tiled=True),
        full_weight,
        preferred_element_type=jnp.float32,
    )
    grad_attention = grad_sum.astype(jnp.bfloat16)
    grad_in = lax.all_to_all(select_rows(to_slot, grad_attention), "seq", 0, 0, tiled=True)
    g_c = select_rows(to_rank, grad_in).reshape(ranks, head_count, HD)

    delta = jnp.sum(g_c.astype(jnp.float32) * attn_c.astype(jnp.float32), axis=2).T[:, :, None]
    dprobs = jnp.einsum("qhd,khd->hqk", g_c, v_c, preferred_element_type=jnp.float32)
    dscores = (probs * (dprobs - delta)).astype(jnp.bfloat16)
    grad_q = (
        jnp.einsum("hqk,khd->qhd", dscores, k_c, preferred_element_type=jnp.float32) * score_scale
    ).astype(jnp.bfloat16)
    grad_k = (
        jnp.einsum("hqk,qhd->khd", dscores, q_c, preferred_element_type=jnp.float32) * score_scale
    ).astype(jnp.bfloat16)
    grad_v = jnp.einsum("hqk,qhd->khd", probs_b, g_c, preferred_element_type=jnp.float32).astype(
        jnp.bfloat16
    )
    grads_c = jnp.concatenate(
        [
            grad_q.reshape(ranks, width),
            grad_k.reshape(ranks, width),
            grad_v.reshape(ranks, width),
        ],
        axis=1,
    )
    grads_back = lax.all_to_all(select_rows_t(to_rank, grads_c), "seq", 0, 0, tiled=True)
    grads_local = select_rows_t(to_slot, grads_back)
    return (
        layer_out,
        grads_local[:, :width],
        grads_local[:, width : 2 * width],
        grads_local[:, 2 * width :],
    )


def solution(mesh):
    in_specs = (
        P("seq", "head"),
        P("seq", "head"),
        P("seq", "head"),
        P("head", "seq"),
        P("seq", "head"),
        P("seq"),
        P(),
    )
    out_specs = (P("seq", "head"), P("seq", "head"), P("seq", "head"), P("seq", "head"))
    return jax.shard_map(
        on_device, mesh=mesh, in_specs=in_specs, out_specs=out_specs, check_vma=False
    )
```

```python
import math

import jax
import jax.numpy as jnp
from jax import lax
from jax.sharding import PartitionSpec as P

HD = 128
BLK = 128


def select_rows(onehot, rows):
    return jnp.dot(onehot, rows, preferred_element_type=jnp.float32).astype(rows.dtype)


def select_rows_t(onehot, rows):
    return lax.dot_general(
        onehot, rows, (((0,), (0,)), ((), ())), preferred_element_type=jnp.float32
    ).astype(rows.dtype)


def ring_gather_cols(block, axis_name, ny, nz, z_first=False):
    index = lax.axis_index(axis_name)
    y = index % ny
    z = index // ny
    n = ny * nz
    cols = block.shape[1]

    def perm(dy, dz):
        return [(i, ((i // ny + dz) % nz) * ny + (i % ny + dy) % ny) for i in range(n)]

    def ring(piece, pos, count, step_perm, width, total):
        out = jnp.zeros((piece.shape[0], total), piece.dtype)
        out = lax.dynamic_update_slice(out, piece, (0, pos * width))
        fwd = piece
        bwd = piece
        for step in range(1, count // 2 + 1):
            fwd = lax.ppermute(fwd, axis_name, step_perm(1))
            out = lax.dynamic_update_slice(out, fwd, (0, ((pos - step) % count) * width))
            if count - step != step:
                bwd = lax.ppermute(bwd, axis_name, step_perm(-1))
                out = lax.dynamic_update_slice(out, bwd, (0, ((pos + step) % count) * width))
        return out

    if not z_first:
        row = ring(block, y, ny, lambda d: perm(d, 0), cols, ny * cols)
        return ring(row, z, nz, lambda d: perm(0, d), ny * cols, n * cols)
    row = ring(block, z, nz, lambda d: perm(0, d), cols, nz * cols)
    full = ring(row, y, ny, lambda d: perm(d, 0), nz * cols, n * cols)
    rows = block.shape[0]
    return full.reshape(rows, ny, nz, cols).transpose(0, 2, 1, 3).reshape(rows, n * cols)


def on_device(queries, key_rows, value_rows, out_weight, grad_output, cluster_ids, block_pattern):
    tokens = queries.shape[0]
    width = queries.shape[1]
    head_count = width // HD
    groups = lax.axis_size("seq")
    slot_rows = 2 * tokens // groups
    slot_total = groups * slot_rows
    ranks = tokens
    owner_index = lax.axis_index("seq")
    score_scale = 1.0 / math.sqrt(HD)

    members = (cluster_ids[:, None] == jnp.arange(groups, dtype=jnp.int32)[None, :]).astype(
        jnp.int32
    )
    earlier = jnp.cumsum(members, axis=0) - members
    local_rank = jnp.sum(earlier * members, axis=1)
    slot_index = cluster_ids * slot_rows + local_rank
    to_slot = (
        jnp.arange(slot_total, dtype=jnp.int32)[:, None] == slot_index[None, :]
    ).astype(jnp.bfloat16)

    ring_y = 4 if groups % 4 == 0 else 1
    half_rows = out_weight.shape[0] // 2
    full_weight = jnp.concatenate(
        [
            ring_gather_cols(out_weight[:half_rows], "seq", ring_y, groups // ring_y),
            ring_gather_cols(out_weight[half_rows:], "seq", ring_y, groups // ring_y, True),
        ],
        axis=0,
    )
    live_flag = jnp.ones((tokens, HD), queries.dtype)
    qkv = jnp.concatenate([queries, key_rows, value_rows, live_flag], axis=1)
    qkv_in = lax.all_to_all(select_rows(to_slot, qkv), "seq", 0, 0, tiled=True)

    row_live = qkv_in[:, 3 * width] > 0.5
    got_counts = jnp.sum(row_live.reshape(groups, slot_rows).astype(jnp.int32), axis=1)
    offsets = jnp.cumsum(got_counts) - got_counts
    place = jnp.arange(slot_rows, dtype=jnp.int32)
    rank_rows = (offsets[:, None] + place[None, :]).reshape(slot_total)
    to_rank = (
        (rank_rows[None, :] == jnp.arange(ranks, dtype=jnp.int32)[:, None]) & row_live[None, :]
    ).astype(jnp.bfloat16)
    qkv_c = select_rows(to_rank, qkv_in)
    q_c = qkv_c[:, :width].reshape(ranks, head_count, HD)
    k_c = qkv_c[:, width : 2 * width].reshape(ranks, head_count, HD)
    v_c = qkv_c[:, 2 * width : 3 * width].reshape(ranks, head_count, HD)

    pattern = lax.dynamic_index_in_dim(block_pattern, owner_index, 0, keepdims=False)
    rank = jnp.arange(ranks, dtype=jnp.int32)
    blk = rank // BLK
    blk_q = blk[:, None]
    blk_k = blk[None, :]
    pat = jnp.where(
        blk_q == 0,
        jnp.where(blk_k == 0, pattern[0, 0], pattern[0, 1]),
        jnp.where(blk_k == 0, pattern[1, 0], pattern[1, 1]),
    )
    allowed = (rank[None, :] <= rank[:, None]) & (pat == 1)

    scores = (
        jnp.einsum("qhd,khd->hqk", q_c, k_c, preferred_element_type=jnp.float32) * score_scale
    )
    scores = jnp.where(allowed[None], scores, -jnp.inf)
    shifted = jnp.exp(scores - jnp.max(scores, axis=2, keepdims=True))
    probs = shifted / jnp.sum(shifted, axis=2, keepdims=True)
    probs_b = probs.astype(jnp.bfloat16)
    attn_c = jnp.einsum("hqk,khd->qhd", probs_b, v_c, preferred_element_type=jnp.float32).astype(
        jnp.bfloat16
    )

    attn_back = lax.all_to_all(
        select_rows_t(to_rank, attn_c.reshape(ranks, width)), "seq", 0, 0, tiled=True
    )
    attn_back, full_weight = lax.optimization_barrier((attn_back, full_weight))
    attn_local = select_rows_t(to_slot, attn_back)
    partial_value = jnp.dot(attn_local, full_weight, preferred_element_type=jnp.float32)
    rounded_part = lax.optimization_barrier(partial_value.astype(jnp.bfloat16)).astype(jnp.float32)
    layer_out = lax.psum_scatter(
        rounded_part.astype(jnp.bfloat16), "head", scatter_dimension=1, tiled=True
    )

    grad_sum = jnp.einsum(
        "td,wd->tw",
        lax.all_gather(grad_output, "head", axis=1, tiled=True),
        full_weight,
        preferred_element_type=jnp.float32,
    )
    grad_attention = grad_sum.astype(jnp.bfloat16)
    grad_in = lax.all_to_all(select_rows(to_slot, grad_attention), "seq", 0, 0, tiled=True)
    g_c = select_rows(to_rank, grad_in).reshape(ranks, head_count, HD)

    delta = jnp.sum(g_c.astype(jnp.float32) * attn_c.astype(jnp.float32), axis=2).T[:, :, None]
    dprobs = jnp.einsum("qhd,khd->hqk", g_c, v_c, preferred_element_type=jnp.float32)
    dscores = (probs * (dprobs - delta)).astype(jnp.bfloat16)
    grad_q = (
        jnp.einsum("hqk,khd->qhd", dscores, k_c, preferred_element_type=jnp.float32) * score_scale
    ).astype(jnp.bfloat16)
    grad_k = (
        jnp.einsum("hqk,qhd->khd", dscores, q_c, preferred_element_type=jnp.float32) * score_scale
    ).astype(jnp.bfloat16)
    grad_v = jnp.einsum("hqk,qhd->khd", probs_b, g_c, preferred_element_type=jnp.float32).astype(
        jnp.bfloat16
    )
    grads_c = jnp.concatenate(
        [
            grad_q.reshape(ranks, width),
            grad_k.reshape(ranks, width),
            grad_v.reshape(ranks, width),
        ],
        axis=1,
    )
    grads_back = lax.all_to_all(select_rows_t(to_rank, grads_c), "seq", 0, 0, tiled=True)
    grads_local = select_rows_t(to_slot, grads_back)
    return (
        layer_out,
        grads_local[:, :width],
        grads_local[:, width : 2 * width],
        grads_local[:, 2 * width :],
    )


def solution(mesh):
    in_specs = (
        P("seq", "head"),
        P("seq", "head"),
        P("seq", "head"),
        P("head", "seq"),
        P("seq", "head"),
        P("seq"),
        P(),
    )
    out_specs = (P("seq", "head"), P("seq", "head"), P("seq", "head"), P("seq", "head"))
    return jax.shard_map(
        on_device, mesh=mesh, in_specs=in_specs, out_specs=out_specs, check_vma=False
    )
```

```python
import math

import jax
import jax.numpy as jnp
from jax import lax
from jax.sharding import PartitionSpec as P

HD = 128
BLK = 128


def select_rows(onehot, rows):
    return jnp.dot(onehot, rows, preferred_element_type=jnp.float32).astype(rows.dtype)


def select_rows_t(onehot, rows):
    return lax.dot_general(
        onehot, rows, (((0,), (0,)), ((), ())), preferred_element_type=jnp.float32
    ).astype(rows.dtype)


def ring_gather_cols(block, axis_name, ny, nz, z_first=False, take=None):
    index = lax.axis_index(axis_name)
    y = index % ny
    z = index // ny
    n = ny * nz
    cols = block.shape[1]

    def perm(dy, dz):
        return [(i, ((i // ny + dz) % nz) * ny + (i % ny + dy) % ny) for i in range(n)]

    def ring(piece, pos, count, step_perm, width, total, use=None):
        out = jnp.zeros((piece.shape[0], total), piece.dtype)
        out = lax.dynamic_update_slice(out, piece, (0, pos * width))
        acc = None if use is None else use(piece, pos)
        fwd = piece
        bwd = piece
        for step in range(1, count // 2 + 1):
            fwd = lax.ppermute(fwd, axis_name, step_perm(1))
            at = (pos - step) % count
            out = lax.dynamic_update_slice(out, fwd, (0, at * width))
            if use is not None:
                acc = acc + use(fwd, at)
            if count - step != step:
                bwd = lax.ppermute(bwd, axis_name, step_perm(-1))
                at = (pos + step) % count
                out = lax.dynamic_update_slice(out, bwd, (0, at * width))
                if use is not None:
                    acc = acc + use(bwd, at)
        return out, acc

    rows = block.shape[0]
    if not z_first:
        row, _ = ring(block, y, ny, lambda d: perm(d, 0), cols, ny * cols)
        return ring(row, z, nz, lambda d: perm(0, d), ny * cols, n * cols, take)
    row, _ = ring(block, z, nz, lambda d: perm(0, d), cols, nz * cols)
    full, acc = ring(row, y, ny, lambda d: perm(d, 0), nz * cols, n * cols, take)
    return full.reshape(rows, ny, nz, cols).transpose(0, 2, 1, 3).reshape(rows, n * cols), acc


def on_device(queries, key_rows, value_rows, out_weight, grad_output, cluster_ids, block_pattern):
    tokens = queries.shape[0]
    width = queries.shape[1]
    head_count = width // HD
    groups = lax.axis_size("seq")
    slot_rows = 2 * tokens // groups
    slot_total = groups * slot_rows
    ranks = tokens
    owner_index = lax.axis_index("seq")
    score_scale = 1.0 / math.sqrt(HD)

    members = (cluster_ids[:, None] == jnp.arange(groups, dtype=jnp.int32)[None, :]).astype(
        jnp.int32
    )
    earlier = jnp.cumsum(members, axis=0) - members
    local_rank = jnp.sum(earlier * members, axis=1)
    slot_index = cluster_ids * slot_rows + local_rank
    to_slot = (
        jnp.arange(slot_total, dtype=jnp.int32)[:, None] == slot_index[None, :]
    ).astype(jnp.bfloat16)

    ring_y = 4 if groups % 4 == 0 else 1
    half_rows = out_weight.shape[0] // 2
    ring_z = groups // ring_y
    cols = out_weight.shape[1]
    grad_full = lax.all_gather(grad_output, "head", axis=1, tiled=True)
    grad_by_y = grad_full.reshape(tokens, ring_z, ring_y, cols)

    def grad_from_zblock(piece, at):
        part = lax.dynamic_slice_in_dim(grad_full, at * ring_y * cols, ring_y * cols, axis=1)
        return jnp.einsum("td,wd->tw", part, piece, preferred_element_type=jnp.float32)

    def grad_from_yblock(piece, at):
        part = lax.dynamic_index_in_dim(grad_by_y, at, axis=2, keepdims=False)
        return jnp.einsum(
            "td,wd->tw", part.reshape(tokens, ring_z * cols), piece,
            preferred_element_type=jnp.float32,
        )

    weight_a, grad_a = ring_gather_cols(
        out_weight[:half_rows], "seq", ring_y, ring_z, False, grad_from_zblock
    )
    weight_b, grad_b = ring_gather_cols(
        out_weight[half_rows:], "seq", ring_y, ring_z, True, grad_from_yblock
    )
    full_weight = jnp.concatenate([weight_a, weight_b], axis=0)
    grad_sum = jnp.concatenate([grad_a, grad_b], axis=1)
    live_flag = jnp.ones((tokens, HD), queries.dtype)
    qkv = jnp.concatenate([queries, key_rows, value_rows, live_flag], axis=1)
    qkv_in = lax.all_to_all(select_rows(to_slot, qkv), "seq", 0, 0, tiled=True)

    row_live = qkv_in[:, 3 * width] > 0.5
    got_counts = jnp.sum(row_live.reshape(groups, slot_rows).astype(jnp.int32), axis=1)
    offsets = jnp.cumsum(got_counts) - got_counts
    place = jnp.arange(slot_rows, dtype=jnp.int32)
    rank_rows = (offsets[:, None] + place[None, :]).reshape(slot_total)
    to_rank = (
        (rank_rows[None, :] == jnp.arange(ranks, dtype=jnp.int32)[:, None]) & row_live[None, :]
    ).astype(jnp.bfloat16)
    qkv_c = select_rows(to_rank, qkv_in)
    q_c = qkv_c[:, :width].reshape(ranks, head_count, HD)
    k_c = qkv_c[:, width : 2 * width].reshape(ranks, head_count, HD)
    v_c = qkv_c[:, 2 * width : 3 * width].reshape(ranks, head_count, HD)

    pattern = lax.dynamic_index_in_dim(block_pattern, owner_index, 0, keepdims=False)
    rank = jnp.arange(ranks, dtype=jnp.int32)
    blk = rank // BLK
    blk_q = blk[:, None]
    blk_k = blk[None, :]
    pat = jnp.where(
        blk_q == 0,
        jnp.where(blk_k == 0, pattern[0, 0], pattern[0, 1]),
        jnp.where(blk_k == 0, pattern[1, 0], pattern[1, 1]),
    )
    allowed = (rank[None, :] <= rank[:, None]) & (pat == 1)

    scores = (
        jnp.einsum("qhd,khd->hqk", q_c, k_c, preferred_element_type=jnp.float32) * score_scale
    )
    scores = jnp.where(allowed[None], scores, -jnp.inf)
    shifted = jnp.exp(scores - jnp.max(scores, axis=2, keepdims=True))
    probs = shifted / jnp.sum(shifted, axis=2, keepdims=True)
    probs_b = probs.astype(jnp.bfloat16)
    attn_c = jnp.einsum("hqk,khd->qhd", probs_b, v_c, preferred_element_type=jnp.float32).astype(
        jnp.bfloat16
    )

    attn_back = lax.all_to_all(
        select_rows_t(to_rank, attn_c.reshape(ranks, width)), "seq", 0, 0, tiled=True
    )
    attn_back, full_weight = lax.optimization_barrier((attn_back, full_weight))
    attn_local = select_rows_t(to_slot, attn_back)
    partial_value = jnp.dot(attn_local, full_weight, preferred_element_type=jnp.float32)
    rounded_part = lax.optimization_barrier(partial_value.astype(jnp.bfloat16)).astype(jnp.float32)
    layer_out = lax.psum_scatter(
        rounded_part.astype(jnp.bfloat16), "head", scatter_dimension=1, tiled=True
    )

    grad_attention = grad_sum.astype(jnp.bfloat16)
    grad_in = lax.all_to_all(select_rows(to_slot, grad_attention), "seq", 0, 0, tiled=True)
    g_c = select_rows(to_rank, grad_in).reshape(ranks, head_count, HD)

    delta = jnp.sum(g_c.astype(jnp.float32) * attn_c.astype(jnp.float32), axis=2).T[:, :, None]
    dprobs = jnp.einsum("qhd,khd->hqk", g_c, v_c, preferred_element_type=jnp.float32)
    dscores = (probs * (dprobs - delta)).astype(jnp.bfloat16)
    grad_q = (
        jnp.einsum("hqk,khd->qhd", dscores, k_c, preferred_element_type=jnp.float32) * score_scale
    ).astype(jnp.bfloat16)
    grad_k = (
        jnp.einsum("hqk,qhd->khd", dscores, q_c, preferred_element_type=jnp.float32) * score_scale
    ).astype(jnp.bfloat16)
    grad_v = jnp.einsum("hqk,qhd->khd", probs_b, g_c, preferred_element_type=jnp.float32).astype(
        jnp.bfloat16
    )
    grads_c = jnp.concatenate(
        [
            grad_q.reshape(ranks, width),
            grad_k.reshape(ranks, width),
            grad_v.reshape(ranks, width),
        ],
        axis=1,
    )
    grads_back = lax.all_to_all(select_rows_t(to_rank, grads_c), "seq", 0, 0, tiled=True)
    grads_local = select_rows_t(to_slot, grads_back)
    return (
        layer_out,
        grads_local[:, :width],
        grads_local[:, width : 2 * width],
        grads_local[:, 2 * width :],
    )


def solution(mesh):
    in_specs = (
        P("seq", "head"),
        P("seq", "head"),
        P("seq", "head"),
        P("head", "seq"),
        P("seq", "head"),
        P("seq"),
        P(),
    )
    out_specs = (P("seq", "head"), P("seq", "head"), P("seq", "head"), P("seq", "head"))
    return jax.shard_map(
        on_device, mesh=mesh, in_specs=in_specs, out_specs=out_specs, check_vma=False
    )
```

```python
import math

import jax
import jax.numpy as jnp
from jax import lax
from jax.sharding import PartitionSpec as P

HD = 128
BLK = 128


def select_rows(onehot, rows):
    return jnp.dot(onehot, rows, preferred_element_type=jnp.float32).astype(rows.dtype)


def select_rows_t(onehot, rows):
    return lax.dot_general(
        onehot, rows, (((0,), (0,)), ((), ())), preferred_element_type=jnp.float32
    ).astype(rows.dtype)


def ring_gather_cols(block, axis_name, ny, nz, z_first=False):
    index = lax.axis_index(axis_name)
    y = index % ny
    z = index // ny
    n = ny * nz
    cols = block.shape[1]

    def perm(dy, dz):
        return [(i, ((i // ny + dz) % nz) * ny + (i % ny + dy) % ny) for i in range(n)]

    def ring(piece, pos, count, step_perm, width, total):
        out = jnp.zeros((piece.shape[0], total), piece.dtype)
        out = lax.dynamic_update_slice(out, piece, (0, pos * width))
        fwd = piece
        bwd = piece
        for step in range(1, count // 2 + 1):
            fwd = lax.ppermute(fwd, axis_name, step_perm(1))
            out = lax.dynamic_update_slice(out, fwd, (0, ((pos - step) % count) * width))
            if count - step != step:
                bwd = lax.ppermute(bwd, axis_name, step_perm(-1))
                out = lax.dynamic_update_slice(out, bwd, (0, ((pos + step) % count) * width))
        return out

    if not z_first:
        row = ring(block, y, ny, lambda d: perm(d, 0), cols, ny * cols)
        return ring(row, z, nz, lambda d: perm(0, d), ny * cols, n * cols)
    row = ring(block, z, nz, lambda d: perm(0, d), cols, nz * cols)
    full = ring(row, y, ny, lambda d: perm(d, 0), nz * cols, n * cols)
    rows = block.shape[0]
    return full.reshape(rows, ny, nz, cols).transpose(0, 2, 1, 3).reshape(rows, n * cols)


def on_device(queries, key_rows, value_rows, out_weight, grad_output, cluster_ids, block_pattern):
    tokens = queries.shape[0]
    width = queries.shape[1]
    head_count = width // HD
    groups = lax.axis_size("seq")
    slot_rows = 2 * tokens // groups
    slot_total = groups * slot_rows
    ranks = tokens
    owner_index = lax.axis_index("seq")
    score_scale = 1.0 / math.sqrt(HD)

    members = (cluster_ids[:, None] == jnp.arange(groups, dtype=jnp.int32)[None, :]).astype(
        jnp.int32
    )
    earlier = jnp.cumsum(members, axis=0) - members
    local_rank = jnp.sum(earlier * members, axis=1)
    slot_index = cluster_ids * slot_rows + local_rank
    to_slot = (
        jnp.arange(slot_total, dtype=jnp.int32)[:, None] == slot_index[None, :]
    ).astype(jnp.bfloat16)

    ring_y = 4 if groups % 4 == 0 else 1
    parts = 4
    part_rows = out_weight.shape[0] // parts
    full_weight = jnp.concatenate(
        [
            ring_gather_cols(
                out_weight[i * part_rows : (i + 1) * part_rows],
                "seq",
                ring_y,
                groups // ring_y,
                i % 2 == 1,
            )
            for i in range(parts)
        ],
        axis=0,
    )
    live_flag = jnp.ones((tokens, HD), queries.dtype)
    qkv = jnp.concatenate([queries, key_rows, value_rows, live_flag], axis=1)
    qkv_in = lax.all_to_all(select_rows(to_slot, qkv), "seq", 0, 0, tiled=True)

    row_live = qkv_in[:, 3 * width] > 0.5
    got_counts = jnp.sum(row_live.reshape(groups, slot_rows).astype(jnp.int32), axis=1)
    offsets = jnp.cumsum(got_counts) - got_counts
    place = jnp.arange(slot_rows, dtype=jnp.int32)
    rank_rows = (offsets[:, None] + place[None, :]).reshape(slot_total)
    to_rank = (
        (rank_rows[None, :] == jnp.arange(ranks, dtype=jnp.int32)[:, None]) & row_live[None, :]
    ).astype(jnp.bfloat16)
    qkv_c = select_rows(to_rank, qkv_in)
    q_c = qkv_c[:, :width].reshape(ranks, head_count, HD)
    k_c = qkv_c[:, width : 2 * width].reshape(ranks, head_count, HD)
    v_c = qkv_c[:, 2 * width : 3 * width].reshape(ranks, head_count, HD)

    pattern = lax.dynamic_index_in_dim(block_pattern, owner_index, 0, keepdims=False)
    rank = jnp.arange(ranks, dtype=jnp.int32)
    blk = rank // BLK
    blk_q = blk[:, None]
    blk_k = blk[None, :]
    pat = jnp.where(
        blk_q == 0,
        jnp.where(blk_k == 0, pattern[0, 0], pattern[0, 1]),
        jnp.where(blk_k == 0, pattern[1, 0], pattern[1, 1]),
    )
    allowed = (rank[None, :] <= rank[:, None]) & (pat == 1)

    scores = (
        jnp.einsum("qhd,khd->hqk", q_c, k_c, preferred_element_type=jnp.float32) * score_scale
    )
    scores = jnp.where(allowed[None], scores, -jnp.inf)
    shifted = jnp.exp(scores - jnp.max(scores, axis=2, keepdims=True))
    probs = shifted / jnp.sum(shifted, axis=2, keepdims=True)
    probs_b = probs.astype(jnp.bfloat16)
    attn_c = jnp.einsum("hqk,khd->qhd", probs_b, v_c, preferred_element_type=jnp.float32).astype(
        jnp.bfloat16
    )

    attn_back = lax.all_to_all(
        select_rows_t(to_rank, attn_c.reshape(ranks, width)), "seq", 0, 0, tiled=True
    )
    attn_back, full_weight = lax.optimization_barrier((attn_back, full_weight))
    attn_local = select_rows_t(to_slot, attn_back)
    partial_value = jnp.dot(attn_local, full_weight, preferred_element_type=jnp.float32)
    rounded_part = lax.optimization_barrier(partial_value.astype(jnp.bfloat16)).astype(jnp.float32)
    layer_out = lax.psum_scatter(
        rounded_part.astype(jnp.bfloat16), "head", scatter_dimension=1, tiled=True
    )

    grad_sum = jnp.einsum(
        "td,wd->tw",
        lax.all_gather(grad_output, "head", axis=1, tiled=True),
        full_weight,
        preferred_element_type=jnp.float32,
    )
    grad_attention = grad_sum.astype(jnp.bfloat16)
    grad_in = lax.all_to_all(select_rows(to_slot, grad_attention), "seq", 0, 0, tiled=True)
    g_c = select_rows(to_rank, grad_in).reshape(ranks, head_count, HD)

    delta = jnp.sum(g_c.astype(jnp.float32) * attn_c.astype(jnp.float32), axis=2).T[:, :, None]
    dprobs = jnp.einsum("qhd,khd->hqk", g_c, v_c, preferred_element_type=jnp.float32)
    dscores = (probs * (dprobs - delta)).astype(jnp.bfloat16)
    grad_q = (
        jnp.einsum("hqk,khd->qhd", dscores, k_c, preferred_element_type=jnp.float32) * score_scale
    ).astype(jnp.bfloat16)
    grad_k = (
        jnp.einsum("hqk,qhd->khd", dscores, q_c, preferred_element_type=jnp.float32) * score_scale
    ).astype(jnp.bfloat16)
    grad_v = jnp.einsum("hqk,qhd->khd", probs_b, g_c, preferred_element_type=jnp.float32).astype(
        jnp.bfloat16
    )
    grads_c = jnp.concatenate(
        [
            grad_q.reshape(ranks, width),
            grad_k.reshape(ranks, width),
            grad_v.reshape(ranks, width),
        ],
        axis=1,
    )
    grads_back = lax.all_to_all(select_rows_t(to_rank, grads_c), "seq", 0, 0, tiled=True)
    grads_local = select_rows_t(to_slot, grads_back)
    return (
        layer_out,
        grads_local[:, :width],
        grads_local[:, width : 2 * width],
        grads_local[:, 2 * width :],
    )


def solution(mesh):
    in_specs = (
        P("seq", "head"),
        P("seq", "head"),
        P("seq", "head"),
        P("head", "seq"),
        P("seq", "head"),
        P("seq"),
        P(),
    )
    out_specs = (P("seq", "head"), P("seq", "head"), P("seq", "head"), P("seq", "head"))
    return jax.shard_map(
        on_device, mesh=mesh, in_specs=in_specs, out_specs=out_specs, check_vma=False
    )
```

```python
import math

import jax
import jax.numpy as jnp
from jax import lax
from jax.sharding import PartitionSpec as P

HD = 128
BLK = 128


def select_rows(onehot, rows):
    return jnp.dot(onehot, rows, preferred_element_type=jnp.float32).astype(rows.dtype)


def select_rows_t(onehot, rows):
    return lax.dot_general(
        onehot, rows, (((0,), (0,)), ((), ())), preferred_element_type=jnp.float32
    ).astype(rows.dtype)


def ring_gather_cols(block, axis_name, ny, nz, z_first=False):
    index = lax.axis_index(axis_name)
    y = index % ny
    z = index // ny
    n = ny * nz
    cols = block.shape[1]

    def perm(dy, dz):
        return [(i, ((i // ny + dz) % nz) * ny + (i % ny + dy) % ny) for i in range(n)]

    def ring(piece, pos, count, step_perm, width, total):
        out = jnp.zeros((piece.shape[0], total), piece.dtype)
        out = lax.dynamic_update_slice(out, piece, (0, pos * width))
        fwd = piece
        bwd = piece
        for step in range(1, count // 2 + 1):
            fwd = lax.ppermute(fwd, axis_name, step_perm(1))
            out = lax.dynamic_update_slice(out, fwd, (0, ((pos - step) % count) * width))
            if count - step != step:
                bwd = lax.ppermute(bwd, axis_name, step_perm(-1))
                out = lax.dynamic_update_slice(out, bwd, (0, ((pos + step) % count) * width))
        return out

    if not z_first:
        row = ring(block, y, ny, lambda d: perm(d, 0), cols, ny * cols)
        return ring(row, z, nz, lambda d: perm(0, d), ny * cols, n * cols)
    row = ring(block, z, nz, lambda d: perm(0, d), cols, nz * cols)
    full = ring(row, y, ny, lambda d: perm(d, 0), nz * cols, n * cols)
    rows = block.shape[0]
    return full.reshape(rows, ny, nz, cols).transpose(0, 2, 1, 3).reshape(rows, n * cols)


def on_device(queries, key_rows, value_rows, out_weight, grad_output, cluster_ids, block_pattern):
    tokens = queries.shape[0]
    width = queries.shape[1]
    head_count = width // HD
    groups = lax.axis_size("seq")
    slot_rows = 2 * tokens // groups
    slot_total = groups * slot_rows
    ranks = tokens
    owner_index = lax.axis_index("seq")
    score_scale = 1.0 / math.sqrt(HD)

    members = (cluster_ids[:, None] == jnp.arange(groups, dtype=jnp.int32)[None, :]).astype(
        jnp.int32
    )
    earlier = jnp.cumsum(members, axis=0) - members
    local_rank = jnp.sum(earlier * members, axis=1)
    slot_index = cluster_ids * slot_rows + local_rank
    to_slot = (
        jnp.arange(slot_total, dtype=jnp.int32)[:, None] == slot_index[None, :]
    ).astype(jnp.bfloat16)

    ring_y = 4 if groups % 4 == 0 else 1
    half_rows = out_weight.shape[0] // 2
    full_weight = jnp.concatenate(
        [
            ring_gather_cols(out_weight[:half_rows], "seq", ring_y, groups // ring_y),
            ring_gather_cols(out_weight[half_rows:], "seq", ring_y, groups // ring_y, True),
        ],
        axis=0,
    )
    live_flag = jnp.ones((tokens, HD), queries.dtype)
    qkv = jnp.concatenate([queries, key_rows, value_rows, live_flag], axis=1)
    qkv_in = lax.all_to_all(select_rows(to_slot, qkv), "seq", 0, 0, tiled=True)

    row_live = qkv_in[:, 3 * width] > 0.5
    got_counts = jnp.sum(row_live.reshape(groups, slot_rows).astype(jnp.int32), axis=1)
    offsets = jnp.cumsum(got_counts) - got_counts
    place = jnp.arange(slot_rows, dtype=jnp.int32)
    rank_rows = (offsets[:, None] + place[None, :]).reshape(slot_total)
    to_rank = (
        (rank_rows[None, :] == jnp.arange(ranks, dtype=jnp.int32)[:, None]) & row_live[None, :]
    ).astype(jnp.bfloat16)
    qkv_c = select_rows(to_rank, qkv_in)
    q_c = qkv_c[:, :width].reshape(ranks, head_count, HD)
    k_c = qkv_c[:, width : 2 * width].reshape(ranks, head_count, HD)
    v_c = qkv_c[:, 2 * width : 3 * width].reshape(ranks, head_count, HD)

    pattern = lax.dynamic_index_in_dim(block_pattern, owner_index, 0, keepdims=False)
    rank = jnp.arange(ranks, dtype=jnp.int32)
    blk = rank // BLK
    blk_q = blk[:, None]
    blk_k = blk[None, :]
    pat = jnp.where(
        blk_q == 0,
        jnp.where(blk_k == 0, pattern[0, 0], pattern[0, 1]),
        jnp.where(blk_k == 0, pattern[1, 0], pattern[1, 1]),
    )
    allowed = (rank[None, :] <= rank[:, None]) & (pat == 1)

    scores = (
        jnp.einsum("qhd,khd->hqk", q_c, k_c, preferred_element_type=jnp.float32) * score_scale
    )
    scores = jnp.where(allowed[None], scores, -jnp.inf)
    shifted = jnp.exp(scores - jnp.max(scores, axis=2, keepdims=True))
    probs = shifted / jnp.sum(shifted, axis=2, keepdims=True)
    probs_b = probs.astype(jnp.bfloat16)
    attn_c = jnp.einsum("hqk,khd->qhd", probs_b, v_c, preferred_element_type=jnp.float32).astype(
        jnp.bfloat16
    )

    grad_sum = jnp.einsum(
        "td,wd->tw",
        lax.all_gather(grad_output, "head", axis=1, tiled=True),
        full_weight,
        preferred_element_type=jnp.float32,
    )
    grad_attention = grad_sum.astype(jnp.bfloat16)
    both = jnp.concatenate(
        [
            select_rows_t(to_rank, attn_c.reshape(ranks, width)),
            select_rows(to_slot, grad_attention),
        ],
        axis=1,
    )
    both_in = lax.all_to_all(both, "seq", 0, 0, tiled=True)
    attn_local = select_rows_t(to_slot, both_in[:, :width])
    partial_value = jnp.dot(attn_local, full_weight, preferred_element_type=jnp.float32)
    rounded_part = lax.optimization_barrier(partial_value.astype(jnp.bfloat16)).astype(jnp.float32)
    layer_out = lax.psum_scatter(
        rounded_part.astype(jnp.bfloat16), "head", scatter_dimension=1, tiled=True
    )
    g_c = select_rows(to_rank, both_in[:, width:]).reshape(ranks, head_count, HD)

    delta = jnp.sum(g_c.astype(jnp.float32) * attn_c.astype(jnp.float32), axis=2).T[:, :, None]
    dprobs = jnp.einsum("qhd,khd->hqk", g_c, v_c, preferred_element_type=jnp.float32)
    dscores = (probs * (dprobs - delta)).astype(jnp.bfloat16)
    grad_q = (
        jnp.einsum("hqk,khd->qhd", dscores, k_c, preferred_element_type=jnp.float32) * score_scale
    ).astype(jnp.bfloat16)
    grad_k = (
        jnp.einsum("hqk,qhd->khd", dscores, q_c, preferred_element_type=jnp.float32) * score_scale
    ).astype(jnp.bfloat16)
    grad_v = jnp.einsum("hqk,qhd->khd", probs_b, g_c, preferred_element_type=jnp.float32).astype(
        jnp.bfloat16
    )
    grads_c = jnp.concatenate(
        [
            grad_q.reshape(ranks, width),
            grad_k.reshape(ranks, width),
            grad_v.reshape(ranks, width),
        ],
        axis=1,
    )
    grads_back = lax.all_to_all(select_rows_t(to_rank, grads_c), "seq", 0, 0, tiled=True)
    grads_local = select_rows_t(to_slot, grads_back)
    return (
        layer_out,
        grads_local[:, :width],
        grads_local[:, width : 2 * width],
        grads_local[:, 2 * width :],
    )


def solution(mesh):
    in_specs = (
        P("seq", "head"),
        P("seq", "head"),
        P("seq", "head"),
        P("head", "seq"),
        P("seq", "head"),
        P("seq"),
        P(),
    )
    out_specs = (P("seq", "head"), P("seq", "head"), P("seq", "head"), P("seq", "head"))
    return jax.shard_map(
        on_device, mesh=mesh, in_specs=in_specs, out_specs=out_specs, check_vma=False
    )
```

```python
import math

import jax
import jax.numpy as jnp
from jax import lax
from jax.sharding import PartitionSpec as P

HD = 128
BLK = 128


def select_rows(onehot, rows):
    return jnp.dot(onehot, rows, preferred_element_type=jnp.float32).astype(rows.dtype)


def select_rows_t(onehot, rows):
    return lax.dot_general(
        onehot, rows, (((0,), (0,)), ((), ())), preferred_element_type=jnp.float32
    ).astype(rows.dtype)


def ring_gather_cols(block, axis_name, ny, nz, z_first=False):
    index = lax.axis_index(axis_name)
    y = index % ny
    z = index // ny
    n = ny * nz
    cols = block.shape[1]

    def perm(dy, dz):
        return [(i, ((i // ny + dz) % nz) * ny + (i % ny + dy) % ny) for i in range(n)]

    def ring(piece, pos, count, step_perm, width, total):
        out = jnp.zeros((piece.shape[0], total), piece.dtype)
        out = lax.dynamic_update_slice(out, piece, (0, pos * width))
        fwd = piece
        bwd = piece
        for step in range(1, count // 2 + 1):
            fwd = lax.ppermute(fwd, axis_name, step_perm(1))
            out = lax.dynamic_update_slice(out, fwd, (0, ((pos - step) % count) * width))
            if count - step != step:
                bwd = lax.ppermute(bwd, axis_name, step_perm(-1))
                out = lax.dynamic_update_slice(out, bwd, (0, ((pos + step) % count) * width))
        return out

    if not z_first:
        row = ring(block, y, ny, lambda d: perm(d, 0), cols, ny * cols)
        return ring(row, z, nz, lambda d: perm(0, d), ny * cols, n * cols)
    row = ring(block, z, nz, lambda d: perm(0, d), cols, nz * cols)
    full = ring(row, y, ny, lambda d: perm(d, 0), nz * cols, n * cols)
    rows = block.shape[0]
    return full.reshape(rows, ny, nz, cols).transpose(0, 2, 1, 3).reshape(rows, n * cols)


def on_device(queries, key_rows, value_rows, out_weight, grad_output, cluster_ids, block_pattern):
    tokens = queries.shape[0]
    width = queries.shape[1]
    head_count = width // HD
    groups = lax.axis_size("seq")
    slot_rows = 2 * tokens // groups
    slot_total = groups * slot_rows
    ranks = tokens
    owner_index = lax.axis_index("seq")
    score_scale = 1.0 / math.sqrt(HD)

    members = (cluster_ids[:, None] == jnp.arange(groups, dtype=jnp.int32)[None, :]).astype(
        jnp.int32
    )
    earlier = jnp.cumsum(members, axis=0) - members
    local_rank = jnp.sum(earlier * members, axis=1)
    slot_index = cluster_ids * slot_rows + local_rank
    to_slot = (
        jnp.arange(slot_total, dtype=jnp.int32)[:, None] == slot_index[None, :]
    ).astype(jnp.bfloat16)

    live_flag = jnp.ones((tokens, HD), queries.dtype)
    qkv = jnp.concatenate([queries, key_rows, value_rows, live_flag], axis=1)
    qkv_in = lax.all_to_all(select_rows(to_slot, qkv), "seq", 0, 0, tiled=True)

    qkv_in, weight_in = lax.optimization_barrier((qkv_in, out_weight))
    ring_y = 4 if groups % 4 == 0 else 1
    half_rows = out_weight.shape[0] // 2
    full_weight = jnp.concatenate(
        [
            ring_gather_cols(weight_in[:half_rows], "seq", ring_y, groups // ring_y),
            ring_gather_cols(weight_in[half_rows:], "seq", ring_y, groups // ring_y, True),
        ],
        axis=0,
    )
    row_live = qkv_in[:, 3 * width] > 0.5
    got_counts = jnp.sum(row_live.reshape(groups, slot_rows).astype(jnp.int32), axis=1)
    offsets = jnp.cumsum(got_counts) - got_counts
    place = jnp.arange(slot_rows, dtype=jnp.int32)
    rank_rows = (offsets[:, None] + place[None, :]).reshape(slot_total)
    to_rank = (
        (rank_rows[None, :] == jnp.arange(ranks, dtype=jnp.int32)[:, None]) & row_live[None, :]
    ).astype(jnp.bfloat16)
    qkv_c = select_rows(to_rank, qkv_in)
    q_c = qkv_c[:, :width].reshape(ranks, head_count, HD)
    k_c = qkv_c[:, width : 2 * width].reshape(ranks, head_count, HD)
    v_c = qkv_c[:, 2 * width : 3 * width].reshape(ranks, head_count, HD)

    pattern = lax.dynamic_index_in_dim(block_pattern, owner_index, 0, keepdims=False)
    rank = jnp.arange(ranks, dtype=jnp.int32)
    blk = rank // BLK
    blk_q = blk[:, None]
    blk_k = blk[None, :]
    pat = jnp.where(
        blk_q == 0,
        jnp.where(blk_k == 0, pattern[0, 0], pattern[0, 1]),
        jnp.where(blk_k == 0, pattern[1, 0], pattern[1, 1]),
    )
    allowed = (rank[None, :] <= rank[:, None]) & (pat == 1)

    scores = (
        jnp.einsum("qhd,khd->hqk", q_c, k_c, preferred_element_type=jnp.float32) * score_scale
    )
    scores = jnp.where(allowed[None], scores, -jnp.inf)
    shifted = jnp.exp(scores - jnp.max(scores, axis=2, keepdims=True))
    probs = shifted / jnp.sum(shifted, axis=2, keepdims=True)
    probs_b = probs.astype(jnp.bfloat16)
    attn_c = jnp.einsum("hqk,khd->qhd", probs_b, v_c, preferred_element_type=jnp.float32).astype(
        jnp.bfloat16
    )

    attn_back = lax.all_to_all(
        select_rows_t(to_rank, attn_c.reshape(ranks, width)), "seq", 0, 0, tiled=True
    )
    attn_back, full_weight = lax.optimization_barrier((attn_back, full_weight))
    attn_local = select_rows_t(to_slot, attn_back)
    partial_value = jnp.dot(attn_local, full_weight, preferred_element_type=jnp.float32)
    rounded_part = lax.optimization_barrier(partial_value.astype(jnp.bfloat16)).astype(jnp.float32)
    layer_out = lax.psum_scatter(
        rounded_part.astype(jnp.bfloat16), "head", scatter_dimension=1, tiled=True
    )

    grad_sum = jnp.einsum(
        "td,wd->tw",
        lax.all_gather(grad_output, "head", axis=1, tiled=True),
        full_weight,
        preferred_element_type=jnp.float32,
    )
    grad_attention = grad_sum.astype(jnp.bfloat16)
    grad_in = lax.all_to_all(select_rows(to_slot, grad_attention), "seq", 0, 0, tiled=True)
    g_c = select_rows(to_rank, grad_in).reshape(ranks, head_count, HD)

    delta = jnp.sum(g_c.astype(jnp.float32) * attn_c.astype(jnp.float32), axis=2).T[:, :, None]
    dprobs = jnp.einsum("qhd,khd->hqk", g_c, v_c, preferred_element_type=jnp.float32)
    dscores = (probs * (dprobs - delta)).astype(jnp.bfloat16)
    grad_q = (
        jnp.einsum("hqk,khd->qhd", dscores, k_c, preferred_element_type=jnp.float32) * score_scale
    ).astype(jnp.bfloat16)
    grad_k = (
        jnp.einsum("hqk,qhd->khd", dscores, q_c, preferred_element_type=jnp.float32) * score_scale
    ).astype(jnp.bfloat16)
    grad_v = jnp.einsum("hqk,qhd->khd", probs_b, g_c, preferred_element_type=jnp.float32).astype(
        jnp.bfloat16
    )
    grads_c = jnp.concatenate(
        [
            grad_q.reshape(ranks, width),
            grad_k.reshape(ranks, width),
            grad_v.reshape(ranks, width),
        ],
        axis=1,
    )
    grads_back = lax.all_to_all(select_rows_t(to_rank, grads_c), "seq", 0, 0, tiled=True)
    grads_local = select_rows_t(to_slot, grads_back)
    return (
        layer_out,
        grads_local[:, :width],
        grads_local[:, width : 2 * width],
        grads_local[:, 2 * width :],
    )


def solution(mesh):
    in_specs = (
        P("seq", "head"),
        P("seq", "head"),
        P("seq", "head"),
        P("head", "seq"),
        P("seq", "head"),
        P("seq"),
        P(),
    )
    out_specs = (P("seq", "head"), P("seq", "head"), P("seq", "head"), P("seq", "head"))
    return jax.shard_map(
        on_device, mesh=mesh, in_specs=in_specs, out_specs=out_specs, check_vma=False
    )
```

```python
import math

import jax
import jax.numpy as jnp
from jax import lax
from jax.sharding import PartitionSpec as P

HD = 128
BLK = 128


def select_rows(onehot, rows):
    return jnp.dot(onehot, rows, preferred_element_type=jnp.float32).astype(rows.dtype)


def select_rows_t(onehot, rows):
    return lax.dot_general(
        onehot, rows, (((0,), (0,)), ((), ())), preferred_element_type=jnp.float32
    ).astype(rows.dtype)


def ring_gather_cols(block, axis_name, ny, nz, z_first=False):
    index = lax.axis_index(axis_name)
    y = index % ny
    z = index // ny
    n = ny * nz
    cols = block.shape[1]

    def perm(dy, dz):
        return [(i, ((i // ny + dz) % nz) * ny + (i % ny + dy) % ny) for i in range(n)]

    def ring(piece, pos, count, step_perm, width, total):
        out = jnp.zeros((piece.shape[0], total), piece.dtype)
        out = lax.dynamic_update_slice(out, piece, (0, pos * width))
        fwd = piece
        bwd = piece
        for step in range(1, count // 2 + 1):
            fwd = lax.ppermute(fwd, axis_name, step_perm(1))
            out = lax.dynamic_update_slice(out, fwd, (0, ((pos - step) % count) * width))
            if count - step != step:
                bwd = lax.ppermute(bwd, axis_name, step_perm(-1))
                out = lax.dynamic_update_slice(out, bwd, (0, ((pos + step) % count) * width))
        return out

    if not z_first:
        row = ring(block, y, ny, lambda d: perm(d, 0), cols, ny * cols)
        return ring(row, z, nz, lambda d: perm(0, d), ny * cols, n * cols)
    row = ring(block, z, nz, lambda d: perm(0, d), cols, nz * cols)
    full = ring(row, y, ny, lambda d: perm(d, 0), nz * cols, n * cols)
    rows = block.shape[0]
    return full.reshape(rows, ny, nz, cols).transpose(0, 2, 1, 3).reshape(rows, n * cols)


def on_device(queries, key_rows, value_rows, out_weight, grad_output, cluster_ids, block_pattern):
    tokens = queries.shape[0]
    width = queries.shape[1]
    head_count = width // HD
    groups = lax.axis_size("seq")
    slot_rows = 2 * tokens // groups
    slot_total = groups * slot_rows
    ranks = tokens
    owner_index = lax.axis_index("seq")
    score_scale = 1.0 / math.sqrt(HD)

    members = (cluster_ids[:, None] == jnp.arange(groups, dtype=jnp.int32)[None, :]).astype(
        jnp.int32
    )
    earlier = jnp.cumsum(members, axis=0) - members
    local_rank = jnp.sum(earlier * members, axis=1)
    slot_index = cluster_ids * slot_rows + local_rank
    to_slot = (
        jnp.arange(slot_total, dtype=jnp.int32)[:, None] == slot_index[None, :]
    ).astype(jnp.bfloat16)

    ring_y = 4 if groups % 4 == 0 else 1
    half_rows = out_weight.shape[0] // 2
    weight_a = ring_gather_cols(out_weight[:half_rows], "seq", ring_y, groups // ring_y)
    weight_b = ring_gather_cols(out_weight[half_rows:], "seq", ring_y, groups // ring_y, True)
    live_flag = jnp.ones((tokens, HD), queries.dtype)
    qkv = jnp.concatenate([queries, key_rows, value_rows, live_flag], axis=1)
    qkv_in = lax.all_to_all(select_rows(to_slot, qkv), "seq", 0, 0, tiled=True)

    row_live = qkv_in[:, 3 * width] > 0.5
    got_counts = jnp.sum(row_live.reshape(groups, slot_rows).astype(jnp.int32), axis=1)
    offsets = jnp.cumsum(got_counts) - got_counts
    place = jnp.arange(slot_rows, dtype=jnp.int32)
    rank_rows = (offsets[:, None] + place[None, :]).reshape(slot_total)
    to_rank = (
        (rank_rows[None, :] == jnp.arange(ranks, dtype=jnp.int32)[:, None]) & row_live[None, :]
    ).astype(jnp.bfloat16)
    qkv_c = select_rows(to_rank, qkv_in)
    q_c = qkv_c[:, :width].reshape(ranks, head_count, HD)
    k_c = qkv_c[:, width : 2 * width].reshape(ranks, head_count, HD)
    v_c = qkv_c[:, 2 * width : 3 * width].reshape(ranks, head_count, HD)

    pattern = lax.dynamic_index_in_dim(block_pattern, owner_index, 0, keepdims=False)
    rank = jnp.arange(ranks, dtype=jnp.int32)
    blk = rank // BLK
    blk_q = blk[:, None]
    blk_k = blk[None, :]
    pat = jnp.where(
        blk_q == 0,
        jnp.where(blk_k == 0, pattern[0, 0], pattern[0, 1]),
        jnp.where(blk_k == 0, pattern[1, 0], pattern[1, 1]),
    )
    allowed = (rank[None, :] <= rank[:, None]) & (pat == 1)

    scores = (
        jnp.einsum("qhd,khd->hqk", q_c, k_c, preferred_element_type=jnp.float32) * score_scale
    )
    scores = jnp.where(allowed[None], scores, -jnp.inf)
    shifted = jnp.exp(scores - jnp.max(scores, axis=2, keepdims=True))
    probs = shifted / jnp.sum(shifted, axis=2, keepdims=True)
    probs_b = probs.astype(jnp.bfloat16)
    attn_c = jnp.einsum("hqk,khd->qhd", probs_b, v_c, preferred_element_type=jnp.float32).astype(
        jnp.bfloat16
    )

    attn_back = lax.all_to_all(
        select_rows_t(to_rank, attn_c.reshape(ranks, width)), "seq", 0, 0, tiled=True
    )
    attn_back, weight_a, weight_b = lax.optimization_barrier((attn_back, weight_a, weight_b))
    attn_local = select_rows_t(to_slot, attn_back)
    partial_value = jnp.dot(
        attn_local[:, :half_rows], weight_a, preferred_element_type=jnp.float32
    ) + jnp.dot(attn_local[:, half_rows:], weight_b, preferred_element_type=jnp.float32)
    rounded_part = lax.optimization_barrier(partial_value.astype(jnp.bfloat16)).astype(jnp.float32)
    layer_out = lax.psum_scatter(
        rounded_part.astype(jnp.bfloat16), "head", scatter_dimension=1, tiled=True
    )

    grad_full = lax.all_gather(grad_output, "head", axis=1, tiled=True)
    grad_sum = jnp.concatenate(
        [
            jnp.einsum("td,wd->tw", grad_full, weight_a, preferred_element_type=jnp.float32),
            jnp.einsum("td,wd->tw", grad_full, weight_b, preferred_element_type=jnp.float32),
        ],
        axis=1,
    )
    grad_attention = grad_sum.astype(jnp.bfloat16)
    grad_in = lax.all_to_all(select_rows(to_slot, grad_attention), "seq", 0, 0, tiled=True)
    g_c = select_rows(to_rank, grad_in).reshape(ranks, head_count, HD)

    delta = jnp.sum(g_c.astype(jnp.float32) * attn_c.astype(jnp.float32), axis=2).T[:, :, None]
    dprobs = jnp.einsum("qhd,khd->hqk", g_c, v_c, preferred_element_type=jnp.float32)
    dscores = (probs * (dprobs - delta)).astype(jnp.bfloat16)
    grad_q = (
        jnp.einsum("hqk,khd->qhd", dscores, k_c, preferred_element_type=jnp.float32) * score_scale
    ).astype(jnp.bfloat16)
    grad_k = (
        jnp.einsum("hqk,qhd->khd", dscores, q_c, preferred_element_type=jnp.float32) * score_scale
    ).astype(jnp.bfloat16)
    grad_v = jnp.einsum("hqk,qhd->khd", probs_b, g_c, preferred_element_type=jnp.float32).astype(
        jnp.bfloat16
    )
    grads_c = jnp.concatenate(
        [
            grad_q.reshape(ranks, width),
            grad_k.reshape(ranks, width),
            grad_v.reshape(ranks, width),
        ],
        axis=1,
    )
    grads_back = lax.all_to_all(select_rows_t(to_rank, grads_c), "seq", 0, 0, tiled=True)
    grads_local = select_rows_t(to_slot, grads_back)
    return (
        layer_out,
        grads_local[:, :width],
        grads_local[:, width : 2 * width],
        grads_local[:, 2 * width :],
    )


def solution(mesh):
    in_specs = (
        P("seq", "head"),
        P("seq", "head"),
        P("seq", "head"),
        P("head", "seq"),
        P("seq", "head"),
        P("seq"),
        P(),
    )
    out_specs = (P("seq", "head"), P("seq", "head"), P("seq", "head"), P("seq", "head"))
    return jax.shard_map(
        on_device, mesh=mesh, in_specs=in_specs, out_specs=out_specs, check_vma=False
    )
```
